512 devices in a mesh: ctx: 32 (over y_lo, z, core), tp: 16 (over x, y_hi).
Axes of the slice: x: 4, y: 8 (y_hi: 4, y_lo: 2; y = y_hi * 2 + y_lo), z: 8, core: 2. Of those that a mesh axis runs over, the one named last changes fastest.
Arguments:
- query: bfloat16 [8192, 4096], P('ctx', 'tp'), may hold values from 0.049804688 to 2
- key_feat: bfloat16 [8192, 4096], P('ctx', 'tp'), may hold values from 0.049804688 to 2
- value: bfloat16 [8192, 4096], P('ctx', 'tp'), may hold values from -36 to 36
- grad_out: bfloat16 [8192, 4096], P('ctx', 'tp'), may hold values from -6 to 6
- w_out: bfloat16 [4096, 4096], P('tp', 'ctx'), may hold values from -0.09375 to 0.09375
Outputs:
- grad_query: bfloat16 [8192, 4096], P('ctx', 'tp')
- grad_key: bfloat16 [8192, 4096], P('ctx', 'tp')
- grad_value: bfloat16 [8192, 4096], P('ctx', 'tp')
The draws below stay inside these ranges and needn't reach their ends.
All inputs are finite; a program needn't handle non-finite values.
Results may differ from the reference program's by a relative error of at most 0.0059.
Values may be sent and summed in bfloat16 or wider, within the bound.
No kernel may reach another device: no remote copies, remote signals or barrier semaphores. Data moves between devices by JAX's collectives and lax.ppermute only.
A program may use at most 64 MiB of HBM per device.

```python
import math
import jax
import jax.numpy as jnp
from jax import lax

D = 4096
E = 128
TOK_DEV = 256
TOKENS = 8192
N_CTX = 32


def draw_value(key, part):
    key_data, key_rows, key_cols = jax.random.split(key, 3)
    row_scale = jnp.exp(jax.random.uniform(key_rows, (TOKENS, 1), jnp.float32, math.log(0.3), math.log(3.0)))
    col_scale = jnp.exp(jax.random.uniform(key_cols, (1, D), jnp.float32, math.log(0.3), math.log(3.0)))
    base = jnp.clip(jax.random.normal(key_data, (TOKENS, D), jnp.float32), -4.0, 4.0)
    return (base * row_scale * col_scale).astype(jnp.bfloat16)


def levels(key, extent, pieces, smallest, largest):
    def one(dim, shards_of):
        draws = jax.random.uniform(jax.random.fold_in(jax.random.fold_in(key, 6), dim), (shards_of,), jnp.float32, smallest / len(pieces), largest / len(pieces))
        return jnp.repeat(jnp.exp(draws), extent[dim] // shards_of).reshape((-1,) + (1,) * (len(extent) - dim - 1))

    loudness = one(*pieces[0])
    for cut in pieces[1:]:
        loudness = loudness * one(*cut)
    return loudness


def gaussian(own_key, dims, scale, bound, pieces=(), dtype=jnp.bfloat16):
    array = scale * jax.random.normal(own_key, dims, jnp.float32)
    if pieces:
        array = array * levels(own_key, dims, pieces, -0.22, 0.18)
    return jnp.clip(array, -bound, bound).astype(dtype)


def setup_inputs(seed: int = 0) -> dict:
    arg_keys = jax.random.split(jax.random.key(seed), 6)
    return {
        "query": jnp.clip(jnp.exp(math.log(2.0) - 3.6927934 * jax.random.uniform(arg_keys[0], (TOKENS, D), jnp.float32) ** levels(arg_keys[0], (TOKENS, D), ((0, 32), (1, 16)), -0.2, 0.2)), 0.049804688, 2.0).astype(jnp.bfloat16),
        "key_feat": jnp.clip(jnp.exp(math.log(2.0) - 3.6927934 * jax.random.uniform(arg_keys[1], (TOKENS, D), jnp.float32) ** levels(arg_keys[1], (TOKENS, D), ((0, 32), (1, 16)), -0.2, 0.2)), 0.049804688, 2.0).astype(jnp.bfloat16),
        "value": draw_value(jax.random.fold_in(arg_keys[5], 71), 0),
        "grad_out": gaussian(arg_keys[3], (TOKENS, D), 1.0, 6.0, ((0, 32), (1, 16))),
        "w_out": gaussian(arg_keys[4], (D, D), D ** -0.5, 0.09375, ((0, 16), (1, 32))),
    }


epsilon = 1e-06
highest = lax.Precision.HIGHEST

def split_heads(matrix):
    return matrix.reshape(N_CTX, TOK_DEV, D // E, E)

def reference(query, key_feat, value, grad_out, w_out):
    grad_z = jnp.dot(grad_out, w_out.T, preferred_element_type=jnp.float32)
    causal = (jnp.arange(TOK_DEV)[:, None] >= jnp.arange(TOK_DEV)[None, :])[None]
    query_blocks = split_heads(query)
    key_blocks = split_heads(key_feat)
    value_blocks = split_heads(value)
    gradz_blocks = split_heads(grad_z)
    zero_state = jnp.zeros((D // E, E, E), jnp.float32)

    def forward(carry_state, block_data):
        query_block, key_block, value_block, gradz_block = block_data
        query_wide = query_block.astype(jnp.float32)
        key_wide = key_block.astype(jnp.float32)
        value_wide = value_block.astype(jnp.float32)
        scores = jnp.einsum('thd,shd->hts', query_wide, key_wide, precision=highest)
        weights = jnp.where(causal, scores, 0.0)
        attended = jnp.einsum('hts,she->the', weights, value_wide, precision=highest)
        attended = attended + jnp.einsum('thd,hde->the', query_wide, carry_state, precision=highest)
        inv_rms = lax.rsqrt(lax.optimization_barrier(jnp.mean(attended * attended, axis=-1, keepdims=True)) + epsilon)
        normed = attended * inv_rms
        grad_att = inv_rms * (gradz_block - normed * lax.optimization_barrier(jnp.mean(gradz_block * normed, axis=-1, keepdims=True)))
        grad_att = grad_att.astype(jnp.bfloat16)
        grad_wide = grad_att.astype(jnp.float32)
        grad_weights = jnp.where(causal, jnp.einsum('the,she->hts', grad_wide, value_wide, precision=highest), 0.0)
        grad_query = jnp.einsum('hts,shd->thd', grad_weights, key_wide, precision=highest)
        grad_query = grad_query + jnp.einsum('the,hde->thd', grad_wide, carry_state, precision=highest)
        carry_state = carry_state + jnp.einsum('shd,she->hde', key_wide, value_wide, precision=highest)
        return (carry_state, (grad_att, grad_query))
    unused, (grad_blocks, grad_query) = lax.scan(forward, zero_state, (query_blocks, key_blocks, value_blocks, gradz_blocks))

    def backward(adjoint, block_data):
        query_block, key_block, value_block, grad_block = block_data
        query_wide = query_block.astype(jnp.float32)
        key_wide = key_block.astype(jnp.float32)
        value_wide = value_block.astype(jnp.float32)
        grad_wide = grad_block.astype(jnp.float32)
        scores = jnp.einsum('thd,shd->hts', query_wide, key_wide, precision=highest)
        weights = jnp.where(causal, scores, 0.0)
        grad_weights = jnp.where(causal, jnp.einsum('the,she->hts', grad_wide, value_wide, precision=highest), 0.0)
        grad_key = jnp.einsum('hts,thd->shd', grad_weights, query_wide, precision=highest)
        grad_key = grad_key + jnp.einsum('she,hde->shd', value_wide, adjoint, precision=highest)
        grad_value = jnp.einsum('hts,the->she', weights, grad_wide, precision=highest)
        grad_value = grad_value + jnp.einsum('shd,hde->she', key_wide, adjoint, precision=highest)
        adjoint = adjoint + jnp.einsum('thd,the->hde', query_wide, grad_wide, precision=highest)
        return (adjoint, (grad_key, grad_value))
    unused_adj, (grad_key, grad_value) = lax.scan(backward, zero_state, (query_blocks, key_blocks, value_blocks, grad_blocks), reverse=True)
    return (grad_query.reshape(TOKENS, D).astype(jnp.bfloat16), grad_key.reshape(TOKENS, D).astype(jnp.bfloat16), grad_value.reshape(TOKENS, D).astype(jnp.bfloat16))
```

```python
import jax
import jax.numpy as jnp
from jax import lax
from jax.sharding import Mesh
from jax.sharding import PartitionSpec as P

E = 128


epsilon = 1e-06
highest = lax.Precision.HIGHEST

CTX = ("ylo", "z", "core")
TP = ("x", "yhi")
CHIPS = ("ylo", "z")


def swap_cores(value):
    return lax.ppermute(value, "core", [(0, 1), (1, 0)])


def ctx_scan(local_state, backward):
    core = lax.axis_index("core")
    other = swap_cores(local_state)
    first = jnp.where(core == 0, local_state, other)
    second = jnp.where(core == 0, other, local_state)
    chip_total = first + second
    if backward:
        within = jnp.where(core == 0, other, jnp.zeros_like(other))
    else:
        within = jnp.where(core == 1, other, jnp.zeros_like(other))
    half = lax.dynamic_index_in_dim(chip_total, core, 0, keepdims=False)
    chips = lax.axis_size("ylo") * lax.axis_size("z")
    window = half
    below = jnp.zeros_like(half)
    distance = 1
    while distance < chips:
        if backward:
            pairs = [(q, q - distance) for q in range(distance, chips)]
        else:
            pairs = [(q, q + distance) for q in range(chips - distance)]
        arrived = lax.ppermute(window, CHIPS, pairs)
        below = below + arrived
        if distance * 2 < chips:
            window = window + arrived
        distance *= 2
    other_half = swap_cores(below)
    head0 = jnp.where(core == 0, below, other_half)
    head1 = jnp.where(core == 0, other_half, below)
    return jnp.stack([head0, head1]) + within


def local(query, key_feat, value, grad_out, w_out):
    tok_rows = query.shape[0]
    feat_width = query.shape[1]
    head_count = feat_width // E
    full_rows = lax.all_gather(grad_out, TP, axis=1, tiled=True)
    grad_z = lax.dot_general(
        full_rows,
        lax.all_gather(w_out, CTX, axis=1, tiled=True),
        (((1,), (1,)), ((), ())),
        preferred_element_type=jnp.float32,
    )
    query_heads = query.reshape(tok_rows, head_count, E)
    key_heads = key_feat.reshape(tok_rows, head_count, E)
    value_heads = value.reshape(tok_rows, head_count, E)
    gradz_heads = grad_z.reshape(tok_rows, head_count, E)
    query_wide = query_heads.astype(jnp.float32)
    key_wide = key_heads.astype(jnp.float32)
    value_wide = value_heads.astype(jnp.float32)
    causal = (
        lax.broadcasted_iota(jnp.int32, (tok_rows, tok_rows), 0)
        >= lax.broadcasted_iota(jnp.int32, (tok_rows, tok_rows), 1)
    )[None]
    scores = jnp.einsum("thd,shd->hts", query_heads, key_heads, preferred_element_type=jnp.float32)
    weights = jnp.where(causal, scores, 0.0)
    local_state = jnp.einsum(
        "shd,she->hde", key_heads, value_heads, preferred_element_type=jnp.float32
    )
    state_in = ctx_scan(local_state, False)
    attended = jnp.einsum("hts,she->the", weights, value_wide, precision=highest)
    attended = attended + jnp.einsum("thd,hde->the", query_wide, state_in, precision=highest)
    inv_rms = lax.rsqrt(jnp.mean(attended * attended, axis=-1, keepdims=True) + epsilon)
    normed = attended * inv_rms
    grad_att = (
        inv_rms * (gradz_heads - normed * jnp.mean(gradz_heads * normed, axis=-1, keepdims=True))
    ).astype(jnp.bfloat16)
    grad_wide = grad_att.astype(jnp.float32)
    grad_weights = jnp.where(
        causal,
        jnp.einsum("the,she->hts", grad_att, value_heads, preferred_element_type=jnp.float32),
        0.0,
    )
    grad_query = jnp.einsum("hts,shd->thd", grad_weights, key_wide, precision=highest)
    grad_query = grad_query + jnp.einsum("the,hde->thd", grad_wide, state_in, precision=highest)
    local_adjoint = jnp.einsum(
        "thd,the->hde", query_heads, grad_att, preferred_element_type=jnp.float32
    )
    adjoint = ctx_scan(local_adjoint, True)
    grad_key = jnp.einsum("hts,thd->shd", grad_weights, query_wide, precision=highest)
    grad_key = grad_key + jnp.einsum("she,hde->shd", value_wide, adjoint, precision=highest)
    grad_value = jnp.einsum("hts,the->she", weights, grad_wide, precision=highest)
    grad_value = grad_value + jnp.einsum("shd,hde->she", key_wide, adjoint, precision=highest)
    return (
        grad_query.reshape(tok_rows, feat_width).astype(jnp.bfloat16),
        grad_key.reshape(tok_rows, feat_width).astype(jnp.bfloat16),
        grad_value.reshape(tok_rows, feat_width).astype(jnp.bfloat16),
    )


def solution(mesh):
    ctx_size, tp_size = mesh.devices.shape
    chips_y = 2
    fine = Mesh(
        mesh.devices.reshape(chips_y, ctx_size // (2 * chips_y), 2, tp_size // 4, 4),
        CTX + TP,
    )
    return jax.shard_map(
        local,
        mesh=fine,
        in_specs=(P(CTX, TP), P(CTX, TP), P(CTX, TP), P(CTX, TP), P(TP, CTX)),
        out_specs=(P(CTX, TP), P(CTX, TP), P(CTX, TP)),
        check_vma=False,
    )
```

```python
import jax
import jax.numpy as jnp
from jax import lax
from jax.sharding import Mesh
from jax.sharding import PartitionSpec as P

E = 128


epsilon = 1e-06
highest = lax.Precision.HIGHEST

CTX = ("ylo", "z", "core")
TP = ("x", "yhi")
CHIPS = ("ylo", "z")


def swap_cores(value):
    return lax.ppermute(value, "core", [(0, 1), (1, 0)])


def ctx_scan(local_state, backward):
    core = lax.axis_index("core")
    other = swap_cores(local_state)
    first = jnp.where(core == 0, local_state, other)
    second = jnp.where(core == 0, other, local_state)
    chip_total = first + second
    if backward:
        within = jnp.where(core == 0, other, jnp.zeros_like(other))
    else:
        within = jnp.where(core == 1, other, jnp.zeros_like(other))
    half = lax.dynamic_index_in_dim(chip_total, core, 0, keepdims=False)
    chips = lax.axis_size("ylo") * lax.axis_size("z")
    window = half
    below = jnp.zeros_like(half)
    distance = 1
    while distance < chips:
        if backward:
            pairs = [(q, q - distance) for q in range(distance, chips)]
        else:
            pairs = [(q, q + distance) for q in range(chips - distance)]
        arrived = lax.ppermute(window, CHIPS, pairs)
        below = below + arrived
        if distance * 2 < chips:
            window = window + arrived
        distance *= 2
    other_half = swap_cores(below)
    head0 = jnp.where(core == 0, below, other_half)
    head1 = jnp.where(core == 0, other_half, below)
    return jnp.stack([head0, head1]) + within


def gather_columns(w_block):
    chips = lax.axis_size("ylo") * lax.axis_size("z")
    spread = jnp.broadcast_to(w_block[None], (chips,) + w_block.shape)
    mine = lax.all_to_all(spread, CHIPS, 0, 0, tiled=True)
    others = swap_cores(mine)
    core = lax.axis_index("core")
    even = jnp.where(core == 0, mine, others)
    odd = jnp.where(core == 0, others, mine)
    return jnp.stack([even, odd], axis=1)


def local(query, key_feat, value, grad_out, w_out):
    tok_rows = query.shape[0]
    feat_width = query.shape[1]
    head_count = feat_width // E
    full_rows = lax.all_gather(grad_out, TP, axis=1, tiled=True)
    columns = gather_columns(w_out)
    grad_z = jnp.einsum(
        "tqrk,qrjk->tj",
        full_rows.reshape(tok_rows, columns.shape[0], 2, columns.shape[3]),
        columns,
        preferred_element_type=jnp.float32,
    )
    query_heads = query.reshape(tok_rows, head_count, E)
    key_heads = key_feat.reshape(tok_rows, head_count, E)
    value_heads = value.reshape(tok_rows, head_count, E)
    gradz_heads = grad_z.reshape(tok_rows, head_count, E)
    query_wide = query_heads.astype(jnp.float32)
    key_wide = key_heads.astype(jnp.float32)
    value_wide = value_heads.astype(jnp.float32)
    causal = (
        lax.broadcasted_iota(jnp.int32, (tok_rows, tok_rows), 0)
        >= lax.broadcasted_iota(jnp.int32, (tok_rows, tok_rows), 1)
    )[None]
    scores = jnp.einsum("thd,shd->hts", query_heads, key_heads, preferred_element_type=jnp.float32)
    weights = jnp.where(causal, scores, 0.0)
    local_state = jnp.einsum(
        "shd,she->hde", key_heads, value_heads, preferred_element_type=jnp.float32
    )
    state_in = ctx_scan(local_state, False)
    attended = jnp.einsum("hts,she->the", weights, value_wide, precision=highest)
    attended = attended + jnp.einsum("thd,hde->the", query_wide, state_in, precision=highest)
    inv_rms = lax.rsqrt(jnp.mean(attended * attended, axis=-1, keepdims=True) + epsilon)
    normed = attended * inv_rms
    grad_att = (
        inv_rms * (gradz_heads - normed * jnp.mean(gradz_heads * normed, axis=-1, keepdims=True))
    ).astype(jnp.bfloat16)
    grad_wide = grad_att.astype(jnp.float32)
    grad_weights = jnp.where(
        causal,
        jnp.einsum("the,she->hts", grad_att, value_heads, preferred_element_type=jnp.float32),
        0.0,
    )
    grad_query = jnp.einsum("hts,shd->thd", grad_weights, key_wide, precision=highest)
    grad_query = grad_query + jnp.einsum("the,hde->thd", grad_wide, state_in, precision=highest)
    local_adjoint = jnp.einsum(
        "thd,the->hde", query_heads, grad_att, preferred_element_type=jnp.float32
    )
    adjoint = ctx_scan(local_adjoint, True)
    grad_key = jnp.einsum("hts,thd->shd", grad_weights, query_wide, precision=highest)
    grad_key = grad_key + jnp.einsum("she,hde->shd", value_wide, adjoint, precision=highest)
    grad_value = jnp.einsum("hts,the->she", weights, grad_wide, precision=highest)
    grad_value = grad_value + jnp.einsum("shd,hde->she", key_wide, adjoint, precision=highest)
    return (
        grad_query.reshape(tok_rows, feat_width).astype(jnp.bfloat16),
        grad_key.reshape(tok_rows, feat_width).astype(jnp.bfloat16),
        grad_value.reshape(tok_rows, feat_width).astype(jnp.bfloat16),
    )


def solution(mesh):
    ctx_size, tp_size = mesh.devices.shape
    chips_y = 2
    fine = Mesh(
        mesh.devices.reshape(chips_y, ctx_size // (2 * chips_y), 2, tp_size // 4, 4),
        CTX + TP,
    )
    return jax.shard_map(
        local,
        mesh=fine,
        in_specs=(P(CTX, TP), P(CTX, TP), P(CTX, TP), P(CTX, TP), P(TP, CTX)),
        out_specs=(P(CTX, TP), P(CTX, TP), P(CTX, TP)),
        check_vma=False,
    )
```

```python
import jax
import jax.numpy as jnp
from jax import lax
from jax.sharding import Mesh
from jax.sharding import PartitionSpec as P

E = 128


epsilon = 1e-06
highest = lax.Precision.HIGHEST

CTX = ("ylo", "z", "core")
TP = ("x", "yhi")
CHIPS = ("ylo", "z")


def swap_cores(value):
    return lax.ppermute(value, "core", [(0, 1), (1, 0)])


def ctx_scan(local_state, backward):
    core = lax.axis_index("core")
    other = swap_cores(local_state)
    first = jnp.where(core == 0, local_state, other)
    second = jnp.where(core == 0, other, local_state)
    chip_total = first + second
    if backward:
        within = jnp.where(core == 0, other, jnp.zeros_like(other))
    else:
        within = jnp.where(core == 1, other, jnp.zeros_like(other))
    half = lax.dynamic_index_in_dim(chip_total, core, 0, keepdims=False)
    chips = lax.axis_size("ylo") * lax.axis_size("z")
    window = half
    below = jnp.zeros_like(half)
    distance = 1
    while distance < chips:
        if backward:
            pairs = [(q, q - distance) for q in range(distance, chips)]
        else:
            pairs = [(q, q + distance) for q in range(chips - distance)]
        arrived = lax.ppermute(window, CHIPS, pairs)
        below = below + arrived
        if distance * 2 < chips:
            window = window + arrived
        distance *= 2
    other_half = swap_cores(below)
    head0 = jnp.where(core == 0, below, other_half)
    head1 = jnp.where(core == 0, other_half, below)
    return jnp.stack([head0, head1]) + within


def gather_columns(w_block):
    chips = lax.axis_size("ylo") * lax.axis_size("z")
    spread = jnp.broadcast_to(w_block[None], (chips,) + w_block.shape)
    mine = lax.all_to_all(spread, CHIPS, 0, 0, tiled=True)
    others = swap_cores(mine)
    core = lax.axis_index("core")
    even = jnp.where(core == 0, mine, others)
    odd = jnp.where(core == 0, others, mine)
    return jnp.stack([even, odd], axis=1)


def local(query, key_feat, value, grad_out, w_out):
    tok_rows = query.shape[0]
    feat_width = query.shape[1]
    head_count = feat_width // E
    tp_size = lax.axis_size("x") * lax.axis_size("yhi")
    spread_rows = jnp.broadcast_to(grad_out[None], (tp_size,) + grad_out.shape)
    full_rows = lax.all_to_all(spread_rows, TP, 0, 0, tiled=True)
    columns = gather_columns(w_out)
    grad_z = jnp.einsum(
        "qtrk,qrjk->tj",
        full_rows.reshape(tp_size, tok_rows, 2, columns.shape[3]),
        columns,
        preferred_element_type=jnp.float32,
    )
    query_heads = query.reshape(tok_rows, head_count, E)
    key_heads = key_feat.reshape(tok_rows, head_count, E)
    value_heads = value.reshape(tok_rows, head_count, E)
    gradz_heads = grad_z.reshape(tok_rows, head_count, E)
    query_wide = query_heads.astype(jnp.float32)
    key_wide = key_heads.astype(jnp.float32)
    value_wide = value_heads.astype(jnp.float32)
    causal = (
        lax.broadcasted_iota(jnp.int32, (tok_rows, tok_rows), 0)
        >= lax.broadcasted_iota(jnp.int32, (tok_rows, tok_rows), 1)
    )[None]
    scores = jnp.einsum("thd,shd->hts", query_heads, key_heads, preferred_element_type=jnp.float32)
    weights = jnp.where(causal, scores, 0.0)
    local_state = jnp.einsum(
        "shd,she->hde", key_heads, value_heads, preferred_element_type=jnp.float32
    )
    state_in = ctx_scan(local_state, False)
    attended = jnp.einsum("hts,she->the", weights, value_wide, precision=highest)
    attended = attended + jnp.einsum("thd,hde->the", query_wide, state_in, precision=highest)
    inv_rms = lax.rsqrt(jnp.mean(attended * attended, axis=-1, keepdims=True) + epsilon)
    normed = attended * inv_rms
    grad_att = (
        inv_rms * (gradz_heads - normed * jnp.mean(gradz_heads * normed, axis=-1, keepdims=True))
    ).astype(jnp.bfloat16)
    grad_wide = grad_att.astype(jnp.float32)
    grad_weights = jnp.where(
        causal,
        jnp.einsum("the,she->hts", grad_att, value_heads, preferred_element_type=jnp.float32),
        0.0,
    )
    grad_query = jnp.einsum("hts,shd->thd", grad_weights, key_wide, precision=highest)
    grad_query = grad_query + jnp.einsum("the,hde->thd", grad_wide, state_in, precision=highest)
    local_adjoint = jnp.einsum(
        "thd,the->hde", query_heads, grad_att, preferred_element_type=jnp.float32
    )
    adjoint = ctx_scan(local_adjoint, True)
    grad_key = jnp.einsum("hts,thd->shd", grad_weights, query_wide, precision=highest)
    grad_key = grad_key + jnp.einsum("she,hde->shd", value_wide, adjoint, precision=highest)
    grad_value = jnp.einsum("hts,the->she", weights, grad_wide, precision=highest)
    grad_value = grad_value + jnp.einsum("shd,hde->she", key_wide, adjoint, precision=highest)
    return (
        grad_query.reshape(tok_rows, feat_width).astype(jnp.bfloat16),
        grad_key.reshape(tok_rows, feat_width).astype(jnp.bfloat16),
        grad_value.reshape(tok_rows, feat_width).astype(jnp.bfloat16),
    )


def solution(mesh):
    ctx_size, tp_size = mesh.devices.shape
    chips_y = 2
    fine = Mesh(
        mesh.devices.reshape(chips_y, ctx_size // (2 * chips_y), 2, tp_size // 4, 4),
        CTX + TP,
    )
    return jax.shard_map(
        local,
        mesh=fine,
        in_specs=(P(CTX, TP), P(CTX, TP), P(CTX, TP), P(CTX, TP), P(TP, CTX)),
        out_specs=(P(CTX, TP), P(CTX, TP), P(CTX, TP)),
        check_vma=False,
    )
```

```python
import jax
import jax.numpy as jnp
from jax import lax
from jax.sharding import Mesh
from jax.sharding import PartitionSpec as P

E = 128


epsilon = 1e-06
highest = lax.Precision.HIGHEST

CTX = ("ylo", "z", "core")
TP = ("x", "yhi")
CHIPS = ("ylo", "z")


def swap_cores(value):
    return lax.ppermute(value, "core", [(0, 1), (1, 0)])


def ctx_scan(local_state, backward):
    core = lax.axis_index("core")
    other = swap_cores(local_state)
    first = jnp.where(core == 0, local_state, other)
    second = jnp.where(core == 0, other, local_state)
    chip_total = first + second
    if backward:
        within = jnp.where(core == 0, other, jnp.zeros_like(other))
    else:
        within = jnp.where(core == 1, other, jnp.zeros_like(other))
    half = lax.dynamic_index_in_dim(chip_total, core, 0, keepdims=False)
    chips = lax.axis_size("ylo") * lax.axis_size("z")
    window = half
    below = jnp.zeros_like(half)
    distance = 1
    while distance < chips:
        if backward:
            pairs = [(q, q - distance) for q in range(distance, chips)]
        else:
            pairs = [(q, q + distance) for q in range(chips - distance)]
        arrived = lax.ppermute(window, CHIPS, pairs)
        below = below + arrived
        if distance * 2 < chips:
            window = window + arrived
        distance *= 2
    other_half = swap_cores(below)
    head0 = jnp.where(core == 0, below, other_half)
    head1 = jnp.where(core == 0, other_half, below)
    return jnp.stack([head0, head1]) + within


def gather_columns(w_block):
    chips = lax.axis_size("ylo") * lax.axis_size("z")
    pieces = [w_block]
    for shift in range(1, chips):
        pieces.append(lax.ppermute(w_block, CHIPS, [(q, (q - shift) % chips) for q in range(chips)]))
    mine = jnp.roll(jnp.stack(pieces), lax.axis_index(CHIPS), axis=0)
    others = swap_cores(mine)
    core = lax.axis_index("core")
    even = jnp.where(core == 0, mine, others)
    odd = jnp.where(core == 0, others, mine)
    return jnp.stack([even, odd], axis=1)


def local(query, key_feat, value, grad_out, w_out):
    tok_rows = query.shape[0]
    feat_width = query.shape[1]
    head_count = feat_width // E
    tp_size = lax.axis_size("x") * lax.axis_size("yhi")
    spread_rows = jnp.broadcast_to(grad_out[None], (tp_size,) + grad_out.shape)
    full_rows = lax.all_to_all(spread_rows, TP, 0, 0, tiled=True)
    columns = gather_columns(w_out)
    grad_z = jnp.einsum(
        "qtrk,qrjk->tj",
        full_rows.reshape(tp_size, tok_rows, 2, columns.shape[3]),
        columns,
        preferred_element_type=jnp.float32,
    )
    query_heads = query.reshape(tok_rows, head_count, E)
    key_heads = key_feat.reshape(tok_rows, head_count, E)
    value_heads = value.reshape(tok_rows, head_count, E)
    gradz_heads = grad_z.reshape(tok_rows, head_count, E)
    query_wide = query_heads.astype(jnp.float32)
    key_wide = key_heads.astype(jnp.float32)
    value_wide = value_heads.astype(jnp.float32)
    causal = (
        lax.broadcasted_iota(jnp.int32, (tok_rows, tok_rows), 0)
        >= lax.broadcasted_iota(jnp.int32, (tok_rows, tok_rows), 1)
    )[None]
    scores = jnp.einsum("thd,shd->hts", query_heads, key_heads, preferred_element_type=jnp.float32)
    weights = jnp.where(causal, scores, 0.0)
    local_state = jnp.einsum(
        "shd,she->hde", key_heads, value_heads, preferred_element_type=jnp.float32
    )
    state_in = ctx_scan(local_state, False)
    attended = jnp.einsum("hts,she->the", weights, value_wide, precision=highest)
    attended = attended + jnp.einsum("thd,hde->the", query_wide, state_in, precision=highest)
    inv_rms = lax.rsqrt(jnp.mean(attended * attended, axis=-1, keepdims=True) + epsilon)
    normed = attended * inv_rms
    grad_att = (
        inv_rms * (gradz_heads - normed * jnp.mean(gradz_heads * normed, axis=-1, keepdims=True))
    ).astype(jnp.bfloat16)
    grad_wide = grad_att.astype(jnp.float32)
    grad_weights = jnp.where(
        causal,
        jnp.einsum("the,she->hts", grad_att, value_heads, preferred_element_type=jnp.float32),
        0.0,
    )
    grad_query = jnp.einsum("hts,shd->thd", grad_weights, key_wide, precision=highest)
    grad_query = grad_query + jnp.einsum("the,hde->thd", grad_wide, state_in, precision=highest)
    local_adjoint = jnp.einsum(
        "thd,the->hde", query_heads, grad_att, preferred_element_type=jnp.float32
    )
    adjoint = ctx_scan(local_adjoint, True)
    grad_key = jnp.einsum("hts,thd->shd", grad_weights, query_wide, precision=highest)
    grad_key = grad_key + jnp.einsum("she,hde->shd", value_wide, adjoint, precision=highest)
    grad_value = jnp.einsum("hts,the->she", weights, grad_wide, precision=highest)
    grad_value = grad_value + jnp.einsum("shd,hde->she", key_wide, adjoint, precision=highest)
    return (
        grad_query.reshape(tok_rows, feat_width).astype(jnp.bfloat16),
        grad_key.reshape(tok_rows, feat_width).astype(jnp.bfloat16),
        grad_value.reshape(tok_rows, feat_width).astype(jnp.bfloat16),
    )


def solution(mesh):
    ctx_size, tp_size = mesh.devices.shape
    chips_y = 2
    fine = Mesh(
        mesh.devices.reshape(chips_y, ctx_size // (2 * chips_y), 2, tp_size // 4, 4),
        CTX + TP,
    )
    return jax.shard_map(
        local,
        mesh=fine,
        in_specs=(P(CTX, TP), P(CTX, TP), P(CTX, TP), P(CTX, TP), P(TP, CTX)),
        out_specs=(P(CTX, TP), P(CTX, TP), P(CTX, TP)),
        check_vma=False,
    )
```

```python
import jax
import jax.numpy as jnp
from jax import lax
from jax.sharding import Mesh
from jax.sharding import PartitionSpec as P

E = 128


epsilon = 1e-06
highest = lax.Precision.HIGHEST

CTX = ("ylo", "z", "core")
TP = ("x", "yhi")
CHIPS = ("ylo", "z")


def swap_cores(value):
    return lax.ppermute(value, "core", [(0, 1), (1, 0)])


def ctx_scan(local_state, backward):
    core = lax.axis_index("core")
    chips = lax.axis_size("ylo") * lax.axis_size("z")
    step = -1 if backward else 1
    nearest = [(q, q + step) for q in range(chips) if 0 <= q + step < chips]
    other = swap_cores(local_state)
    own_head = lax.dynamic_index_in_dim(local_state, core, 0, keepdims=False)
    cross_head = lax.dynamic_index_in_dim(local_state, 1 - core, 0, keepdims=False)
    same = lax.ppermute(own_head, CHIPS, nearest)
    cross = lax.ppermute(
        cross_head, CTX, [(2 * q + c, 2 * t + 1 - c) for q, t in nearest for c in (0, 1)]
    )
    below = jnp.where(core == 0, same + cross, cross + same)
    paired = lax.dynamic_index_in_dim(other, core, 0, keepdims=False)
    window = jnp.where(core == 0, own_head + paired, paired + own_head) + below
    if backward:
        within = jnp.where(core == 0, other, jnp.zeros_like(other))
    else:
        within = jnp.where(core == 1, other, jnp.zeros_like(other))
    distance = 2
    while distance < chips:
        pairs = [(q, q + step * distance) for q in range(chips) if 0 <= q + step * distance < chips]
        arrived = lax.ppermute(window, CHIPS, pairs)
        below = below + arrived
        if distance * 2 < chips:
            window = window + arrived
        distance *= 2
    other_half = swap_cores(below)
    head0 = jnp.where(core == 0, below, other_half)
    head1 = jnp.where(core == 0, other_half, below)
    return jnp.stack([head0, head1]) + within


def gather_columns(w_block):
    chips = lax.axis_size("ylo") * lax.axis_size("z")
    spread = jnp.broadcast_to(w_block[None], (chips,) + w_block.shape)
    mine = lax.all_to_all(spread, CHIPS, 0, 0, tiled=True)
    others = swap_cores(mine)
    core = lax.axis_index("core")
    even = jnp.where(core == 0, mine, others)
    odd = jnp.where(core == 0, others, mine)
    return jnp.stack([even, odd], axis=1)


def local(query, key_feat, value, grad_out, w_out):
    tok_rows = query.shape[0]
    feat_width = query.shape[1]
    head_count = feat_width // E
    full_rows = lax.all_gather(grad_out, TP, axis=1, tiled=True)
    columns = gather_columns(w_out)
    grad_z = jnp.einsum(
        "tqrk,qrjk->tj",
        full_rows.reshape(tok_rows, columns.shape[0], 2, columns.shape[3]),
        columns,
        preferred_element_type=jnp.float32,
    )
    query_heads = query.reshape(tok_rows, head_count, E)
    key_heads = key_feat.reshape(tok_rows, head_count, E)
    value_heads = value.reshape(tok_rows, head_count, E)
    gradz_heads = grad_z.reshape(tok_rows, head_count, E)
    query_wide = query_heads.astype(jnp.float32)
    key_wide = key_heads.astype(jnp.float32)
    value_wide = value_heads.astype(jnp.float32)
    causal = (
        lax.broadcasted_iota(jnp.int32, (tok_rows, tok_rows), 0)
        >= lax.broadcasted_iota(jnp.int32, (tok_rows, tok_rows), 1)
    )[None]
    scores = jnp.einsum("thd,shd->hts", query_heads, key_heads, preferred_element_type=jnp.float32)
    weights = jnp.where(causal, scores, 0.0)
    local_state = jnp.einsum(
        "shd,she->hde", key_heads, value_heads, preferred_element_type=jnp.float32
    )
    state_in = ctx_scan(local_state, False)
    attended = jnp.einsum("hts,she->the", weights, value_wide, precision=highest)
    attended = attended + jnp.einsum("thd,hde->the", query_wide, state_in, precision=highest)
    inv_rms = lax.rsqrt(jnp.mean(attended * attended, axis=-1, keepdims=True) + epsilon)
    normed = attended * inv_rms
    grad_att = (
        inv_rms * (gradz_heads - normed * jnp.mean(gradz_heads * normed, axis=-1, keepdims=True))
    ).astype(jnp.bfloat16)
    grad_wide = grad_att.astype(jnp.float32)
    grad_weights = jnp.where(
        causal,
        jnp.einsum("the,she->hts", grad_att, value_heads, preferred_element_type=jnp.float32),
        0.0,
    )
    grad_query = jnp.einsum("hts,shd->thd", grad_weights, key_wide, precision=highest)
    grad_query = grad_query + jnp.einsum("the,hde->thd", grad_wide, state_in, precision=highest)
    local_adjoint = jnp.einsum(
        "thd,the->hde", query_heads, grad_att, preferred_element_type=jnp.float32
    )
    adjoint = ctx_scan(local_adjoint, True)
    grad_key = jnp.einsum("hts,thd->shd", grad_weights, query_wide, precision=highest)
    grad_key = grad_key + jnp.einsum("she,hde->shd", value_wide, adjoint, precision=highest)
    grad_value = jnp.einsum("hts,the->she", weights, grad_wide, precision=highest)
    grad_value = grad_value + jnp.einsum("shd,hde->she", key_wide, adjoint, precision=highest)
    return (
        grad_query.reshape(tok_rows, feat_width).astype(jnp.bfloat16),
        grad_key.reshape(tok_rows, feat_width).astype(jnp.bfloat16),
        grad_value.reshape(tok_rows, feat_width).astype(jnp.bfloat16),
    )


def solution(mesh):
    ctx_size, tp_size = mesh.devices.shape
    chips_y = 2
    fine = Mesh(
        mesh.devices.reshape(chips_y, ctx_size // (2 * chips_y), 2, tp_size // 4, 4),
        CTX + TP,
    )
    return jax.shard_map(
        local,
        mesh=fine,
        in_specs=(P(CTX, TP), P(CTX, TP), P(CTX, TP), P(CTX, TP), P(TP, CTX)),
        out_specs=(P(CTX, TP), P(CTX, TP), P(CTX, TP)),
        check_vma=False,
    )
```

```python
import jax
import jax.numpy as jnp
from jax import lax
from jax.sharding import Mesh
from jax.sharding import PartitionSpec as P

E = 128


epsilon = 1e-06
highest = lax.Precision.HIGHEST

CTX = ("ylo", "z", "core")
TP = ("x", "yhi")
CHIPS = ("ylo", "z")


def swap_cores(value):
    return lax.ppermute(value, "core", [(0, 1), (1, 0)])


def ctx_scan(local_state, backward):
    core = lax.axis_index("core")
    other = swap_cores(local_state)
    first = jnp.where(core == 0, local_state, other)
    second = jnp.where(core == 0, other, local_state)
    chip_total = first + second
    if backward:
        within = jnp.where(core == 0, other, jnp.zeros_like(other))
    else:
        within = jnp.where(core == 1, other, jnp.zeros_like(other))
    half = lax.dynamic_index_in_dim(chip_total, core, 0, keepdims=False)
    chips = lax.axis_size("ylo") * lax.axis_size("z")
    spread = jnp.broadcast_to(half[None], (chips,) + half.shape)
    totals = lax.all_to_all(spread, CHIPS, 0, 0, tiled=True)
    order = lax.broadcasted_iota(jnp.int32, (chips, 1, 1), 0)
    here = lax.axis_index(CHIPS)
    taken = order > here if backward else order < here
    below = jnp.sum(jnp.where(taken, totals, 0.0), axis=0)
    other_half = swap_cores(below)
    head0 = jnp.where(core == 0, below, other_half)
    head1 = jnp.where(core == 0, other_half, below)
    return jnp.stack([head0, head1]) + within


def gather_columns(w_block):
    chips = lax.axis_size("ylo") * lax.axis_size("z")
    spread = jnp.broadcast_to(w_block[None], (chips,) + w_block.shape)
    mine = lax.all_to_all(spread, CHIPS, 0, 0, tiled=True)
    others = swap_cores(mine)
    core = lax.axis_index("core")
    even = jnp.where(core == 0, mine, others)
    odd = jnp.where(core == 0, others, mine)
    return jnp.stack([even, odd], axis=1)


def local(query, key_feat, value, grad_out, w_out):
    tok_rows = query.shape[0]
    feat_width = query.shape[1]
    head_count = feat_width // E
    full_rows = lax.all_gather(grad_out, TP, axis=1, tiled=True)
    columns = gather_columns(w_out)
    grad_z = jnp.einsum(
        "tqrk,qrjk->tj",
        full_rows.reshape(tok_rows, columns.shape[0], 2, columns.shape[3]),
        columns,
        preferred_element_type=jnp.float32,
    )
    query_heads = query.reshape(tok_rows, head_count, E)
    key_heads = key_feat.reshape(tok_rows, head_count, E)
    value_heads = value.reshape(tok_rows, head_count, E)
    gradz_heads = grad_z.reshape(tok_rows, head_count, E)
    query_wide = query_heads.astype(jnp.float32)
    key_wide = key_heads.astype(jnp.float32)
    value_wide = value_heads.astype(jnp.float32)
    causal = (
        lax.broadcasted_iota(jnp.int32, (tok_rows, tok_rows), 0)
        >= lax.broadcasted_iota(jnp.int32, (tok_rows, tok_rows), 1)
    )[None]
    scores = jnp.einsum("thd,shd->hts", query_heads, key_heads, preferred_element_type=jnp.float32)
    weights = jnp.where(causal, scores, 0.0)
    local_state = jnp.einsum(
        "shd,she->hde", key_heads, value_heads, preferred_element_type=jnp.float32
    )
    state_in = ctx_scan(local_state, False)
    attended = jnp.einsum("hts,she->the", weights, value_wide, precision=highest)
    attended = attended + jnp.einsum("thd,hde->the", query_wide, state_in, precision=highest)
    inv_rms = lax.rsqrt(jnp.mean(attended * attended, axis=-1, keepdims=True) + epsilon)
    normed = attended * inv_rms
    grad_att = (
        inv_rms * (gradz_heads - normed * jnp.mean(gradz_heads * normed, axis=-1, keepdims=True))
    ).astype(jnp.bfloat16)
    grad_wide = grad_att.astype(jnp.float32)
    grad_weights = jnp.where(
        causal,
        jnp.einsum("the,she->hts", grad_att, value_heads, preferred_element_type=jnp.float32),
        0.0,
    )
    grad_query = jnp.einsum("hts,shd->thd", grad_weights, key_wide, precision=highest)
    grad_query = grad_query + jnp.einsum("the,hde->thd", grad_wide, state_in, precision=highest)
    local_adjoint = jnp.einsum(
        "thd,the->hde", query_heads, grad_att, preferred_element_type=jnp.float32
    )
    adjoint = ctx_scan(local_adjoint, True)
    grad_key = jnp.einsum("hts,thd->shd", grad_weights, query_wide, precision=highest)
    grad_key = grad_key + jnp.einsum("she,hde->shd", value_wide, adjoint, precision=highest)
    grad_value = jnp.einsum("hts,the->she", weights, grad_wide, precision=highest)
    grad_value = grad_value + jnp.einsum("shd,hde->she", key_wide, adjoint, precision=highest)
    return (
        grad_query.reshape(tok_rows, feat_width).astype(jnp.bfloat16),
        grad_key.reshape(tok_rows, feat_width).astype(jnp.bfloat16),
        grad_value.reshape(tok_rows, feat_width).astype(jnp.bfloat16),
    )


def solution(mesh):
    ctx_size, tp_size = mesh.devices.shape
    chips_y = 2
    fine = Mesh(
        mesh.devices.reshape(chips_y, ctx_size // (2 * chips_y), 2, tp_size // 4, 4),
        CTX + TP,
    )
    return jax.shard_map(
        local,
        mesh=fine,
        in_specs=(P(CTX, TP), P(CTX, TP), P(CTX, TP), P(CTX, TP), P(TP, CTX)),
        out_specs=(P(CTX, TP), P(CTX, TP), P(CTX, TP)),
        check_vma=False,
    )
```

```python
import jax
import jax.numpy as jnp
from jax import lax
from jax.sharding import Mesh
from jax.sharding import PartitionSpec as P

E = 128


epsilon = 1e-06
highest = lax.Precision.HIGHEST

CTX = ("ylo", "z", "core")
TP = ("x", "yhi")
CHIPS = ("ylo", "z")


def swap_cores(value):
    return lax.ppermute(value, "core", [(0, 1), (1, 0)])


def ctx_scan(local_state, backward):
    core = lax.axis_index("core")
    other = swap_cores(local_state)
    first = jnp.where(core == 0, local_state, other)
    second = jnp.where(core == 0, other, local_state)
    chip_total = first + second
    if backward:
        within = jnp.where(core == 0, other, jnp.zeros_like(other))
    else:
        within = jnp.where(core == 1, other, jnp.zeros_like(other))
    half = lax.dynamic_index_in_dim(chip_total, core, 0, keepdims=False)
    chips = lax.axis_size("ylo") * lax.axis_size("z")
    window = half
    below = jnp.zeros_like(half)
    distance = 1
    while distance < chips:
        if backward:
            pairs = [(q, q - distance) for q in range(distance, chips)]
        else:
            pairs = [(q, q + distance) for q in range(chips - distance)]
        arrived = lax.ppermute(window, CHIPS, pairs)
        below = below + arrived
        if distance * 2 < chips:
            window = window + arrived
        distance *= 2
    other_half = swap_cores(below)
    head0 = jnp.where(core == 0, below, other_half)
    head1 = jnp.where(core == 0, other_half, below)
    return jnp.stack([head0, head1]) + within


def place_rows(w_block):
    z_size, y_groups = lax.axis_size("z"), lax.axis_size("yhi")
    pairs = []
    for ylo in range(lax.axis_size("ylo")):
        for z in range(z_size):
            for core in range(2):
                for yhi in range(y_groups):
                    if z % y_groups != yhi:
                        target_z = (z // y_groups) * y_groups + yhi
                        source = ((ylo * z_size + z) * 2 + core) * y_groups + yhi
                        target = ((ylo * z_size + target_z) * 2 + core) * y_groups + z % y_groups
                        pairs.append((source, target))
    moved = lax.ppermute(w_block, ("ylo", "z", "core", "yhi"), pairs)
    kept = lax.axis_index("z") % y_groups == lax.axis_index("yhi")
    return jnp.where(kept, w_block, moved)


def gather_columns(w_block):
    chips = lax.axis_size("ylo") * lax.axis_size("z")
    spread = jnp.broadcast_to(w_block[None], (chips,) + w_block.shape)
    mine = lax.all_to_all(spread, CHIPS, 0, 0, tiled=True)
    others = swap_cores(mine)
    core = lax.axis_index("core")
    even = jnp.where(core == 0, mine, others)
    odd = jnp.where(core == 0, others, mine)
    return jnp.stack([even, odd], axis=1)


def output_gradient(grad_out, w_out):
    x_size, y_groups = lax.axis_size("x"), lax.axis_size("yhi")
    spread_rows = jnp.broadcast_to(grad_out[None], (x_size,) + grad_out.shape)
    rows = lax.all_to_all(spread_rows, "x", 0, 0, tiled=True)
    columns = gather_columns(place_rows(w_out))
    columns = columns.reshape((x_size, y_groups) + columns.shape[1:])
    tok_rows = grad_out.shape[0]
    partial = jnp.einsum(
        "atrk,abrjk->btj",
        rows.reshape(x_size, tok_rows, 2, columns.shape[-1]),
        columns,
        preferred_element_type=jnp.float32,
    )
    parts = lax.all_to_all(partial, "yhi", 0, 0, tiled=True)
    return jnp.sum(parts, axis=0)


def local(query, key_feat, value, grad_out, w_out):
    tok_rows = query.shape[0]
    feat_width = query.shape[1]
    head_count = feat_width // E
    grad_z = output_gradient(grad_out, w_out)
    query_heads = query.reshape(tok_rows, head_count, E)
    key_heads = key_feat.reshape(tok_rows, head_count, E)
    value_heads = value.reshape(tok_rows, head_count, E)
    gradz_heads = grad_z.reshape(tok_rows, head_count, E)
    query_wide = query_heads.astype(jnp.float32)
    key_wide = key_heads.astype(jnp.float32)
    value_wide = value_heads.astype(jnp.float32)
    causal = (
        lax.broadcasted_iota(jnp.int32, (tok_rows, tok_rows), 0)
        >= lax.broadcasted_iota(jnp.int32, (tok_rows, tok_rows), 1)
    )[None]
    scores = jnp.einsum("thd,shd->hts", query_heads, key_heads, preferred_element_type=jnp.float32)
    weights = jnp.where(causal, scores, 0.0)
    local_state = jnp.einsum(
        "shd,she->hde", key_heads, value_heads, preferred_element_type=jnp.float32
    )
    state_in = ctx_scan(local_state, False)
    attended = jnp.einsum("hts,she->the", weights, value_wide, precision=highest)
    attended = attended + jnp.einsum("thd,hde->the", query_wide, state_in, precision=highest)
    inv_rms = lax.rsqrt(jnp.mean(attended * attended, axis=-1, keepdims=True) + epsilon)
    normed = attended * inv_rms
    grad_att = (
        inv_rms * (gradz_heads - normed * jnp.mean(gradz_heads * normed, axis=-1, keepdims=True))
    ).astype(jnp.bfloat16)
    grad_wide = grad_att.astype(jnp.float32)
    grad_weights = jnp.where(
        causal,
        jnp.einsum("the,she->hts", grad_att, value_heads, preferred_element_type=jnp.float32),
        0.0,
    )
    grad_query = jnp.einsum("hts,shd->thd", grad_weights, key_wide, precision=highest)
    grad_query = grad_query + jnp.einsum("the,hde->thd", grad_wide, state_in, precision=highest)
    local_adjoint = jnp.einsum(
        "thd,the->hde", query_heads, grad_att, preferred_element_type=jnp.float32
    )
    adjoint = ctx_scan(local_adjoint, True)
    grad_key = jnp.einsum("hts,thd->shd", grad_weights, query_wide, precision=highest)
    grad_key = grad_key + jnp.einsum("she,hde->shd", value_wide, adjoint, precision=highest)
    grad_value = jnp.einsum("hts,the->she", weights, grad_wide, precision=highest)
    grad_value = grad_value + jnp.einsum("shd,hde->she", key_wide, adjoint, precision=highest)
    return (
        grad_query.reshape(tok_rows, feat_width).astype(jnp.bfloat16),
        grad_key.reshape(tok_rows, feat_width).astype(jnp.bfloat16),
        grad_value.reshape(tok_rows, feat_width).astype(jnp.bfloat16),
    )


def solution(mesh):
    ctx_size, tp_size = mesh.devices.shape
    chips_y = 2
    fine = Mesh(
        mesh.devices.reshape(chips_y, ctx_size // (2 * chips_y), 2, tp_size // 4, 4),
        CTX + TP,
    )
    return jax.shard_map(
        local,
        mesh=fine,
        in_specs=(P(CTX, TP), P(CTX, TP), P(CTX, TP), P(CTX, TP), P(TP, CTX)),
        out_specs=(P(CTX, TP), P(CTX, TP), P(CTX, TP)),
        check_vma=False,
    )
```

```python
import jax
import jax.numpy as jnp
from jax import lax
from jax.sharding import Mesh
from jax.sharding import PartitionSpec as P

E = 128


epsilon = 1e-06
highest = lax.Precision.HIGHEST

CTX = ("ylo", "z", "core")
TP = ("x", "yhi")
CHIPS = ("ylo", "z")


def swap_cores(value):
    return lax.ppermute(value, "core", [(0, 1), (1, 0)])


def ctx_scan(local_state, backward):
    core = lax.axis_index("core")
    other = swap_cores(local_state)
    first = jnp.where(core == 0, local_state, other)
    second = jnp.where(core == 0, other, local_state)
    chip_total = first + second
    if backward:
        within = jnp.where(core == 0, other, jnp.zeros_like(other))
    else:
        within = jnp.where(core == 1, other, jnp.zeros_like(other))
    half = lax.dynamic_index_in_dim(chip_total, core, 0, keepdims=False)
    chips = lax.axis_size("ylo") * lax.axis_size("z")
    window = half
    below = jnp.zeros_like(half)
    distance = 1
    while distance < chips:
        if backward:
            pairs = [(q, q - distance) for q in range(distance, chips)]
        else:
            pairs = [(q, q + distance) for q in range(chips - distance)]
        arrived = lax.ppermute(window, CHIPS, pairs)
        below = below + arrived
        if distance * 2 < chips:
            window = window + arrived
        distance *= 2
    other_half = swap_cores(below)
    head0 = jnp.where(core == 0, below, other_half)
    head1 = jnp.where(core == 0, other_half, below)
    return jnp.stack([head0, head1]) + within


def place_rows(w_block):
    z_size, y_groups = lax.axis_size("z"), lax.axis_size("yhi")
    pairs = []
    for ylo in range(lax.axis_size("ylo")):
        for z in range(z_size):
            for core in range(2):
                for yhi in range(y_groups):
                    if z % y_groups != yhi:
                        target_z = (z // y_groups) * y_groups + yhi
                        source = ((ylo * z_size + z) * 2 + core) * y_groups + yhi
                        target = ((ylo * z_size + target_z) * 2 + core) * y_groups + z % y_groups
                        pairs.append((source, target))
    moved = lax.ppermute(w_block, ("ylo", "z", "core", "yhi"), pairs)
    kept = lax.axis_index("z") % y_groups == lax.axis_index("yhi")
    return jnp.where(kept, w_block, moved)


def gather_columns(w_block):
    chips = lax.axis_size("ylo") * lax.axis_size("z")
    spread = jnp.broadcast_to(w_block[None], (chips,) + w_block.shape)
    mine = lax.all_to_all(spread, CHIPS, 0, 0, tiled=True)
    others = swap_cores(mine)
    core = lax.axis_index("core")
    even = jnp.where(core == 0, mine, others)
    odd = jnp.where(core == 0, others, mine)
    return jnp.stack([even, odd], axis=1)


def output_gradient(grad_out, w_out):
    x_size, y_groups = lax.axis_size("x"), lax.axis_size("yhi")
    here = lax.axis_index("x")
    shifted = [grad_out] + [
        lax.ppermute(grad_out, "x", [(i, (i - shift) % x_size) for i in range(x_size)])
        for shift in range(1, x_size)
    ]
    rows = jnp.roll(jnp.stack(shifted), here, axis=0)
    columns = gather_columns(place_rows(w_out))
    columns = columns.reshape((x_size, y_groups) + columns.shape[1:])
    tok_rows = grad_out.shape[0]
    partial = jnp.einsum(
        "atrk,abrjk->btj",
        rows.reshape(x_size, tok_rows, 2, columns.shape[-1]),
        columns,
        preferred_element_type=jnp.float32,
    )
    parts = lax.all_to_all(partial, "yhi", 0, 0, tiled=True)
    return jnp.sum(parts, axis=0)


def local(query, key_feat, value, grad_out, w_out):
    tok_rows = query.shape[0]
    feat_width = query.shape[1]
    head_count = feat_width // E
    grad_z = output_gradient(grad_out, w_out)
    query_heads = query.reshape(tok_rows, head_count, E)
    key_heads = key_feat.reshape(tok_rows, head_count, E)
    value_heads = value.reshape(tok_rows, head_count, E)
    gradz_heads = grad_z.reshape(tok_rows, head_count, E)
    query_wide = query_heads.astype(jnp.float32)
    key_wide = key_heads.astype(jnp.float32)
    value_wide = value_heads.astype(jnp.float32)
    causal = (
        lax.broadcasted_iota(jnp.int32, (tok_rows, tok_rows), 0)
        >= lax.broadcasted_iota(jnp.int32, (tok_rows, tok_rows), 1)
    )[None]
    scores = jnp.einsum("thd,shd->hts", query_heads, key_heads, preferred_element_type=jnp.float32)
    weights = jnp.where(causal, scores, 0.0)
    local_state = jnp.einsum(
        "shd,she->hde", key_heads, value_heads, preferred_element_type=jnp.float32
    )
    state_in = ctx_scan(local_state, False)
    attended = jnp.einsum("hts,she->the", weights, value_wide, precision=highest)
    attended = attended + jnp.einsum("thd,hde->the", query_wide, state_in, precision=highest)
    inv_rms = lax.rsqrt(jnp.mean(attended * attended, axis=-1, keepdims=True) + epsilon)
    normed = attended * inv_rms
    grad_att = (
        inv_rms * (gradz_heads - normed * jnp.mean(gradz_heads * normed, axis=-1, keepdims=True))
    ).astype(jnp.bfloat16)
    grad_wide = grad_att.astype(jnp.float32)
    grad_weights = jnp.where(
        causal,
        jnp.einsum("the,she->hts", grad_att, value_heads, preferred_element_type=jnp.float32),
        0.0,
    )
    grad_query = jnp.einsum("hts,shd->thd", grad_weights, key_wide, precision=highest)
    grad_query = grad_query + jnp.einsum("the,hde->thd", grad_wide, state_in, precision=highest)
    local_adjoint = jnp.einsum(
        "thd,the->hde", query_heads, grad_att, preferred_element_type=jnp.float32
    )
    adjoint = ctx_scan(local_adjoint, True)
    grad_key = jnp.einsum("hts,thd->shd", grad_weights, query_wide, precision=highest)
    grad_key = grad_key + jnp.einsum("she,hde->shd", value_wide, adjoint, precision=highest)
    grad_value = jnp.einsum("hts,the->she", weights, grad_wide, precision=highest)
    grad_value = grad_value + jnp.einsum("shd,hde->she", key_wide, adjoint, precision=highest)
    return (
        grad_query.reshape(tok_rows, feat_width).astype(jnp.bfloat16),
        grad_key.reshape(tok_rows, feat_width).astype(jnp.bfloat16),
        grad_value.reshape(tok_rows, feat_width).astype(jnp.bfloat16),
    )


def solution(mesh):
    ctx_size, tp_size = mesh.devices.shape
    chips_y = 2
    fine = Mesh(
        mesh.devices.reshape(chips_y, ctx_size // (2 * chips_y), 2, tp_size // 4, 4),
        CTX + TP,
    )
    return jax.shard_map(
        local,
        mesh=fine,
        in_specs=(P(CTX, TP), P(CTX, TP), P(CTX, TP), P(CTX, TP), P(TP, CTX)),
        out_specs=(P(CTX, TP), P(CTX, TP), P(CTX, TP)),
        check_vma=False,
    )
```

```python
import jax
import jax.numpy as jnp
from jax import lax
from jax.sharding import Mesh
from jax.sharding import PartitionSpec as P

E = 128


epsilon = 1e-06
highest = lax.Precision.HIGHEST

CTX = ("ylo", "z", "core")
TP = ("x", "yhi")
CHIPS = ("ylo", "z")


def swap_cores(value):
    return lax.ppermute(value, "core", [(0, 1), (1, 0)])


def ctx_scan(local_state, backward, hold=None):
    core = lax.axis_index("core")
    other = swap_cores(local_state)
    first = jnp.where(core == 0, local_state, other)
    second = jnp.where(core == 0, other, local_state)
    chip_total = first + second
    if backward:
        within = jnp.where(core == 0, other, jnp.zeros_like(other))
    else:
        within = jnp.where(core == 1, other, jnp.zeros_like(other))
    half = lax.dynamic_index_in_dim(chip_total, core, 0, keepdims=False)
    chips = lax.axis_size("ylo") * lax.axis_size("z")
    window = half
    below = jnp.zeros_like(half)
    distance = 1
    while distance < chips:
        if backward:
            pairs = [(q, q - distance) for q in range(distance, chips)]
        else:
            pairs = [(q, q + distance) for q in range(chips - distance)]
        arrived = lax.ppermute(window, CHIPS, pairs)
        below = below + arrived
        if distance * 2 < chips:
            window = window + arrived
        if hold is not None and distance == 2:
            window, below, hold = lax.optimization_barrier((window, below, hold))
        distance *= 2
    other_half = swap_cores(below)
    head0 = jnp.where(core == 0, below, other_half)
    head1 = jnp.where(core == 0, other_half, below)
    return jnp.stack([head0, head1]) + within, hold


def place_rows(w_block):
    z_size, y_groups = lax.axis_size("z"), lax.axis_size("yhi")
    pairs = []
    for ylo in range(lax.axis_size("ylo")):
        for z in range(z_size):
            for core in range(2):
                for yhi in range(y_groups):
                    if z % y_groups != yhi:
                        target_z = (z // y_groups) * y_groups + yhi
                        source = ((ylo * z_size + z) * 2 + core) * y_groups + yhi
                        target = ((ylo * z_size + target_z) * 2 + core) * y_groups + z % y_groups
                        pairs.append((source, target))
    moved = lax.ppermute(w_block, ("ylo", "z", "core", "yhi"), pairs)
    kept = lax.axis_index("z") % y_groups == lax.axis_index("yhi")
    return jnp.where(kept, w_block, moved)


def gather_columns(w_block):
    chips = lax.axis_size("ylo") * lax.axis_size("z")
    spread = jnp.broadcast_to(w_block[None], (chips,) + w_block.shape)
    mine = lax.all_to_all(spread, CHIPS, 0, 0, tiled=True)
    others = swap_cores(mine)
    core = lax.axis_index("core")
    even = jnp.where(core == 0, mine, others)
    odd = jnp.where(core == 0, others, mine)
    return jnp.stack([even, odd], axis=1)


def output_gradient(grad_out, placed):
    x_size, y_groups = lax.axis_size("x"), lax.axis_size("yhi")
    here = lax.axis_index("x")
    shifted = [grad_out] + [
        lax.ppermute(grad_out, "x", [(i, (i - shift) % x_size) for i in range(x_size)])
        for shift in range(1, x_size)
    ]
    rows = jnp.roll(jnp.stack(shifted), here, axis=0)
    columns = gather_columns(placed)
    columns = columns.reshape((x_size, y_groups) + columns.shape[1:])
    tok_rows = grad_out.shape[0]
    partial = jnp.einsum(
        "atrk,abrjk->btj",
        rows.reshape(x_size, tok_rows, 2, columns.shape[-1]),
        columns,
        preferred_element_type=jnp.float32,
    )
    parts = lax.all_to_all(partial, "yhi", 0, 0, tiled=True)
    return jnp.sum(parts, axis=0)


def local(query, key_feat, value, grad_out, w_out):
    tok_rows = query.shape[0]
    feat_width = query.shape[1]
    head_count = feat_width // E
    placed = place_rows(w_out)
    query_heads = query.reshape(tok_rows, head_count, E)
    key_heads = key_feat.reshape(tok_rows, head_count, E)
    value_heads = value.reshape(tok_rows, head_count, E)
    query_wide = query_heads.astype(jnp.float32)
    key_wide = key_heads.astype(jnp.float32)
    value_wide = value_heads.astype(jnp.float32)
    causal = (
        lax.broadcasted_iota(jnp.int32, (tok_rows, tok_rows), 0)
        >= lax.broadcasted_iota(jnp.int32, (tok_rows, tok_rows), 1)
    )[None]
    scores = jnp.einsum("thd,shd->hts", query_heads, key_heads, preferred_element_type=jnp.float32)
    weights = jnp.where(causal, scores, 0.0)
    local_state = jnp.einsum(
        "shd,she->hde", key_heads, value_heads, preferred_element_type=jnp.float32
    )
    state_in, placed = ctx_scan(local_state, False, placed)
    grad_z = output_gradient(grad_out, placed)
    gradz_heads = grad_z.reshape(tok_rows, head_count, E)
    attended = jnp.einsum("hts,she->the", weights, value_wide, precision=highest)
    attended = attended + jnp.einsum("thd,hde->the", query_wide, state_in, precision=highest)
    inv_rms = lax.rsqrt(jnp.mean(attended * attended, axis=-1, keepdims=True) + epsilon)
    normed = attended * inv_rms
    grad_att = (
        inv_rms * (gradz_heads - normed * jnp.mean(gradz_heads * normed, axis=-1, keepdims=True))
    ).astype(jnp.bfloat16)
    grad_wide = grad_att.astype(jnp.float32)
    grad_weights = jnp.where(
        causal,
        jnp.einsum("the,she->hts", grad_att, value_heads, preferred_element_type=jnp.float32),
        0.0,
    )
    grad_query = jnp.einsum("hts,shd->thd", grad_weights, key_wide, precision=highest)
    grad_query = grad_query + jnp.einsum("the,hde->thd", grad_wide, state_in, precision=highest)
    local_adjoint = jnp.einsum(
        "thd,the->hde", query_heads, grad_att, preferred_element_type=jnp.float32
    )
    adjoint, _ = ctx_scan(local_adjoint, True)
    grad_key = jnp.einsum("hts,thd->shd", grad_weights, query_wide, precision=highest)
    grad_key = grad_key + jnp.einsum("she,hde->shd", value_wide, adjoint, precision=highest)
    grad_value = jnp.einsum("hts,the->she", weights, grad_wide, precision=highest)
    grad_value = grad_value + jnp.einsum("shd,hde->she", key_wide, adjoint, precision=highest)
    return (
        grad_query.reshape(tok_rows, feat_width).astype(jnp.bfloat16),
        grad_key.reshape(tok_rows, feat_width).astype(jnp.bfloat16),
        grad_value.reshape(tok_rows, feat_width).astype(jnp.bfloat16),
    )


def solution(mesh):
    ctx_size, tp_size = mesh.devices.shape
    chips_y = 2
    fine = Mesh(
        mesh.devices.reshape(chips_y, ctx_size // (2 * chips_y), 2, tp_size // 4, 4),
        CTX + TP,
    )
    return jax.shard_map(
        local,
        mesh=fine,
        in_specs=(P(CTX, TP), P(CTX, TP), P(CTX, TP), P(CTX, TP), P(TP, CTX)),
        out_specs=(P(CTX, TP), P(CTX, TP), P(CTX, TP)),
        check_vma=False,
    )
```

```python
import jax
import jax.numpy as jnp
from jax import lax
from jax.sharding import Mesh
from jax.sharding import PartitionSpec as P

E = 128


epsilon = 1e-06
highest = lax.Precision.HIGHEST

CTX = ("ylo", "z", "core")
TP = ("x", "yhi")
CHIPS = ("ylo", "z")


def swap_cores(value):
    return lax.ppermute(value, "core", [(0, 1), (1, 0)])


def ctx_scan(local_state, backward, hold=None):
    core = lax.axis_index("core")
    chips = lax.axis_size("ylo") * lax.axis_size("z")
    step = -1 if backward else 1
    nearest = [(q, q + step) for q in range(chips) if 0 <= q + step < chips]
    other = swap_cores(local_state)
    own_head = lax.dynamic_index_in_dim(local_state, core, 0, keepdims=False)
    cross_head = lax.dynamic_index_in_dim(local_state, 1 - core, 0, keepdims=False)
    same = lax.ppermute(own_head, CHIPS, nearest)
    cross = lax.ppermute(
        cross_head, CTX, [(2 * q + c, 2 * t + 1 - c) for q, t in nearest for c in (0, 1)]
    )
    below = jnp.where(core == 0, same + cross, cross + same)
    paired = lax.dynamic_index_in_dim(other, core, 0, keepdims=False)
    window = jnp.where(core == 0, own_head + paired, paired + own_head) + below
    if backward:
        within = jnp.where(core == 0, other, jnp.zeros_like(other))
    else:
        within = jnp.where(core == 1, other, jnp.zeros_like(other))
    distance = 2
    while distance < chips:
        pairs = [(q, q + step * distance) for q in range(chips) if 0 <= q + step * distance < chips]
        arrived = lax.ppermute(window, CHIPS, pairs)
        below = below + arrived
        if distance * 2 < chips:
            window = window + arrived
        if hold is not None and distance == 4:
            window, below, hold = lax.optimization_barrier((window, below, hold))
        distance *= 2
    other_half = swap_cores(below)
    head0 = jnp.where(core == 0, below, other_half)
    head1 = jnp.where(core == 0, other_half, below)
    return jnp.stack([head0, head1]) + within, hold


def gather_columns(w_block):
    chips = lax.axis_size("ylo") * lax.axis_size("z")
    spread = jnp.broadcast_to(w_block[None], (chips,) + w_block.shape)
    mine = lax.all_to_all(spread, CHIPS, 0, 0, tiled=True)
    others = swap_cores(mine)
    core = lax.axis_index("core")
    even = jnp.where(core == 0, mine, others)
    odd = jnp.where(core == 0, others, mine)
    return jnp.stack([even, odd], axis=1)


def local(query, key_feat, value, grad_out, w_out):
    tok_rows = query.shape[0]
    feat_width = query.shape[1]
    head_count = feat_width // E
    full_rows = lax.all_gather(grad_out, TP, axis=1, tiled=True)
    key_heads = key_feat.reshape(tok_rows, head_count, E)
    value_heads = value.reshape(tok_rows, head_count, E)
    local_state = jnp.einsum(
        "shd,she->hde", key_heads, value_heads, preferred_element_type=jnp.float32
    )
    state_in, w_held = ctx_scan(local_state, False, w_out)
    columns = gather_columns(w_held)
    grad_z = jnp.einsum(
        "tqrk,qrjk->tj",
        full_rows.reshape(tok_rows, columns.shape[0], 2, columns.shape[3]),
        columns,
        preferred_element_type=jnp.float32,
    )
    query_heads = query.reshape(tok_rows, head_count, E)
    key_heads = key_feat.reshape(tok_rows, head_count, E)
    value_heads = value.reshape(tok_rows, head_count, E)
    gradz_heads = grad_z.reshape(tok_rows, head_count, E)
    query_wide = query_heads.astype(jnp.float32)
    key_wide = key_heads.astype(jnp.float32)
    value_wide = value_heads.astype(jnp.float32)
    causal = (
        lax.broadcasted_iota(jnp.int32, (tok_rows, tok_rows), 0)
        >= lax.broadcasted_iota(jnp.int32, (tok_rows, tok_rows), 1)
    )[None]
    scores = jnp.einsum("thd,shd->hts", query_heads, key_heads, preferred_element_type=jnp.float32)
    weights = jnp.where(causal, scores, 0.0)
    attended = jnp.einsum("hts,she->the", weights, value_wide, precision=highest)
    attended = attended + jnp.einsum("thd,hde->the", query_wide, state_in, precision=highest)
    inv_rms = lax.rsqrt(jnp.mean(attended * attended, axis=-1, keepdims=True) + epsilon)
    normed = attended * inv_rms
    grad_att = (
        inv_rms * (gradz_heads - normed * jnp.mean(gradz_heads * normed, axis=-1, keepdims=True))
    ).astype(jnp.bfloat16)
    grad_wide = grad_att.astype(jnp.float32)
    grad_weights = jnp.where(
        causal,
        jnp.einsum("the,she->hts", grad_att, value_heads, preferred_element_type=jnp.float32),
        0.0,
    )
    grad_query = jnp.einsum("hts,shd->thd", grad_weights, key_wide, precision=highest)
    grad_query = grad_query + jnp.einsum("the,hde->thd", grad_wide, state_in, precision=highest)
    local_adjoint = jnp.einsum(
        "thd,the->hde", query_heads, grad_att, preferred_element_type=jnp.float32
    )
    adjoint, _ = ctx_scan(local_adjoint, True)
    grad_key = jnp.einsum("hts,thd->shd", grad_weights, query_wide, precision=highest)
    grad_key = grad_key + jnp.einsum("she,hde->shd", value_wide, adjoint, precision=highest)
    grad_value = jnp.einsum("hts,the->she", weights, grad_wide, precision=highest)
    grad_value = grad_value + jnp.einsum("shd,hde->she", key_wide, adjoint, precision=highest)
    return (
        grad_query.reshape(tok_rows, feat_width).astype(jnp.bfloat16),
        grad_key.reshape(tok_rows, feat_width).astype(jnp.bfloat16),
        grad_value.reshape(tok_rows, feat_width).astype(jnp.bfloat16),
    )


def solution(mesh):
    ctx_size, tp_size = mesh.devices.shape
    chips_y = 2
    fine = Mesh(
        mesh.devices.reshape(chips_y, ctx_size // (2 * chips_y), 2, tp_size // 4, 4),
        CTX + TP,
    )
    return jax.shard_map(
        local,
        mesh=fine,
        in_specs=(P(CTX, TP), P(CTX, TP), P(CTX, TP), P(CTX, TP), P(TP, CTX)),
        out_specs=(P(CTX, TP), P(CTX, TP), P(CTX, TP)),
        check_vma=False,
    )
```

```python
import jax
import jax.numpy as jnp
from jax import lax
from jax.sharding import Mesh
from jax.sharding import PartitionSpec as P

E = 128


epsilon = 1e-06
highest = lax.Precision.HIGHEST

CTX = ("ylo", "z", "core")
TP = ("x", "yhi")
CHIPS = ("ylo", "z")


def swap_cores(value):
    return lax.ppermute(value, "core", [(0, 1), (1, 0)])


def ctx_scan(local_state, backward):
    core = lax.axis_index("core")
    other = swap_cores(local_state)
    first = jnp.where(core == 0, local_state, other)
    second = jnp.where(core == 0, other, local_state)
    chip_total = first + second
    if backward:
        within = jnp.where(core == 0, other, jnp.zeros_like(other))
    else:
        within = jnp.where(core == 1, other, jnp.zeros_like(other))
    half = lax.dynamic_index_in_dim(chip_total, core, 0, keepdims=False)
    chips = lax.axis_size("ylo") * lax.axis_size("z")
    window = half
    below = jnp.zeros_like(half)
    distance = 1
    while distance < chips:
        if backward:
            pairs = [(q, q - distance) for q in range(distance, chips)]
        else:
            pairs = [(q, q + distance) for q in range(chips - distance)]
        arrived = lax.ppermute(window, CHIPS, pairs)
        below = below + arrived
        if distance * 2 < chips:
            window = window + arrived
        distance *= 2
    other_half = swap_cores(below)
    head0 = jnp.where(core == 0, below, other_half)
    head1 = jnp.where(core == 0, other_half, below)
    return jnp.stack([head0, head1]) + within


def gather_columns(w_block):
    chips = lax.axis_size("ylo") * lax.axis_size("z")
    spread = jnp.broadcast_to(w_block[None], (chips,) + w_block.shape)
    mine = lax.all_to_all(spread, CHIPS, 0, 0, tiled=True)
    others = swap_cores(mine)
    core = lax.axis_index("core")
    even = jnp.where(core == 0, mine, others)
    odd = jnp.where(core == 0, others, mine)
    return jnp.stack([even, odd], axis=1)


def local(query, key_feat, value, grad_out, w_out):
    tok_rows = query.shape[0]
    feat_width = query.shape[1]
    head_count = feat_width // E
    full_rows = lax.all_gather(grad_out, TP, axis=1, tiled=True)
    columns = gather_columns(w_out)
    query_heads = query.reshape(tok_rows, head_count, E)
    key_heads = key_feat.reshape(tok_rows, head_count, E)
    value_heads = value.reshape(tok_rows, head_count, E)
    query_wide = query_heads.astype(jnp.float32)
    key_wide = key_heads.astype(jnp.float32)
    value_wide = value_heads.astype(jnp.float32)
    causal = (
        lax.broadcasted_iota(jnp.int32, (tok_rows, tok_rows), 0)
        >= lax.broadcasted_iota(jnp.int32, (tok_rows, tok_rows), 1)
    )[None]
    scores = jnp.einsum("thd,shd->hts", query_heads, key_heads, preferred_element_type=jnp.float32)
    weights = jnp.where(causal, scores, 0.0)
    local_state = jnp.einsum(
        "shd,she->hde", key_heads, value_heads, preferred_element_type=jnp.float32
    )
    columns, local_state = lax.optimization_barrier((columns, local_state))
    state_in = ctx_scan(local_state, False)
    grad_z = jnp.einsum(
        "tqrk,qrjk->tj",
        full_rows.reshape(tok_rows, columns.shape[0], 2, columns.shape[3]),
        columns,
        preferred_element_type=jnp.float32,
    )
    gradz_heads = grad_z.reshape(tok_rows, head_count, E)
    attended = jnp.einsum("hts,she->the", weights, value_wide, precision=highest)
    attended = attended + jnp.einsum("thd,hde->the", query_wide, state_in, precision=highest)
    inv_rms = lax.rsqrt(jnp.mean(attended * attended, axis=-1, keepdims=True) + epsilon)
    normed = attended * inv_rms
    grad_att = (
        inv_rms * (gradz_heads - normed * jnp.mean(gradz_heads * normed, axis=-1, keepdims=True))
    ).astype(jnp.bfloat16)
    grad_wide = grad_att.astype(jnp.float32)
    grad_weights = jnp.where(
        causal,
        jnp.einsum("the,she->hts", grad_att, value_heads, preferred_element_type=jnp.float32),
        0.0,
    )
    grad_query = jnp.einsum("hts,shd->thd", grad_weights, key_wide, precision=highest)
    grad_query = grad_query + jnp.einsum("the,hde->thd", grad_wide, state_in, precision=highest)
    local_adjoint = jnp.einsum(
        "thd,the->hde", query_heads, grad_att, preferred_element_type=jnp.float32
    )
    adjoint = ctx_scan(local_adjoint, True)
    grad_key = jnp.einsum("hts,thd->shd", grad_weights, query_wide, precision=highest)
    grad_key = grad_key + jnp.einsum("she,hde->shd", value_wide, adjoint, precision=highest)
    grad_value = jnp.einsum("hts,the->she", weights, grad_wide, precision=highest)
    grad_value = grad_value + jnp.einsum("shd,hde->she", key_wide, adjoint, precision=highest)
    return (
        grad_query.reshape(tok_rows, feat_width).astype(jnp.bfloat16),
        grad_key.reshape(tok_rows, feat_width).astype(jnp.bfloat16),
        grad_value.reshape(tok_rows, feat_width).astype(jnp.bfloat16),
    )


def solution(mesh):
    ctx_size, tp_size = mesh.devices.shape
    chips_y = 2
    fine = Mesh(
        mesh.devices.reshape(chips_y, ctx_size // (2 * chips_y), 2, tp_size // 4, 4),
        CTX + TP,
    )
    return jax.shard_map(
        local,
        mesh=fine,
        in_specs=(P(CTX, TP), P(CTX, TP), P(CTX, TP), P(CTX, TP), P(TP, CTX)),
        out_specs=(P(CTX, TP), P(CTX, TP), P(CTX, TP)),
        check_vma=False,
    )
```

```python
import jax
import jax.numpy as jnp
from jax import lax
from jax.sharding import Mesh
from jax.sharding import PartitionSpec as P

E = 128


epsilon = 1e-06
highest = lax.Precision.HIGHEST

CTX = ("ylo", "z", "core")
TP = ("x", "yhi")
CHIPS = ("ylo", "z")


def swap_cores(value):
    return lax.ppermute(value, "core", [(0, 1), (1, 0)])


def ctx_scan(local_state, backward):
    core = lax.axis_index("core")
    other = swap_cores(local_state)
    first = jnp.where(core == 0, local_state, other)
    second = jnp.where(core == 0, other, local_state)
    chip_total = first + second
    if backward:
        within = jnp.where(core == 0, other, jnp.zeros_like(other))
    else:
        within = jnp.where(core == 1, other, jnp.zeros_like(other))
    half = lax.dynamic_index_in_dim(chip_total, core, 0, keepdims=False)
    chips = lax.axis_size("ylo") * lax.axis_size("z")
    window = half
    below = jnp.zeros_like(half)
    distance = 1
    while distance < chips:
        if backward:
            pairs = [(q, q - distance) for q in range(distance, chips)]
        else:
            pairs = [(q, q + distance) for q in range(chips - distance)]
        arrived = lax.ppermute(window, CHIPS, pairs)
        below = below + arrived
        if distance * 2 < chips:
            window = window + arrived
        distance *= 2
    other_half = swap_cores(below)
    head0 = jnp.where(core == 0, below, other_half)
    head1 = jnp.where(core == 0, other_half, below)
    return jnp.stack([head0, head1]) + within


def merged_scan(local_state, backward):
    core = lax.axis_index("core")
    chips = lax.axis_size("ylo") * lax.axis_size("z")
    step = -1 if backward else 1
    nearest = [(q, q + step) for q in range(chips) if 0 <= q + step < chips]
    other = swap_cores(local_state)
    own_head = lax.dynamic_index_in_dim(local_state, core, 0, keepdims=False)
    cross_head = lax.dynamic_index_in_dim(local_state, 1 - core, 0, keepdims=False)
    same = lax.ppermute(own_head, CHIPS, nearest)
    cross = lax.ppermute(
        cross_head, CTX, [(2 * q + c, 2 * t + 1 - c) for q, t in nearest for c in (0, 1)]
    )
    below = jnp.where(core == 0, same + cross, cross + same)
    paired = lax.dynamic_index_in_dim(other, core, 0, keepdims=False)
    window = jnp.where(core == 0, own_head + paired, paired + own_head) + below
    if backward:
        within = jnp.where(core == 0, other, jnp.zeros_like(other))
    else:
        within = jnp.where(core == 1, other, jnp.zeros_like(other))
    distance = 2
    while distance < chips:
        pairs = [(q, q + step * distance) for q in range(chips) if 0 <= q + step * distance < chips]
        arrived = lax.ppermute(window, CHIPS, pairs)
        below = below + arrived
        if distance * 2 < chips:
            window = window + arrived
        distance *= 2
    other_half = swap_cores(below)
    head0 = jnp.where(core == 0, below, other_half)
    head1 = jnp.where(core == 0, other_half, below)
    return jnp.stack([head0, head1]) + within


def gather_columns(w_block):
    chips = lax.axis_size("ylo") * lax.axis_size("z")
    spread = jnp.broadcast_to(w_block[None], (chips,) + w_block.shape)
    mine = lax.all_to_all(spread, CHIPS, 0, 0, tiled=True)
    others = swap_cores(mine)
    core = lax.axis_index("core")
    even = jnp.where(core == 0, mine, others)
    odd = jnp.where(core == 0, others, mine)
    return jnp.stack([even, odd], axis=1)


def local(query, key_feat, value, grad_out, w_out):
    tok_rows = query.shape[0]
    feat_width = query.shape[1]
    head_count = feat_width // E
    full_rows = lax.all_gather(grad_out, TP, axis=1, tiled=True)
    columns = gather_columns(w_out)
    grad_z = jnp.einsum(
        "tqrk,qrjk->tj",
        full_rows.reshape(tok_rows, columns.shape[0], 2, columns.shape[3]),
        columns,
        preferred_element_type=jnp.float32,
    )
    query_heads = query.reshape(tok_rows, head_count, E)
    key_heads = key_feat.reshape(tok_rows, head_count, E)
    value_heads = value.reshape(tok_rows, head_count, E)
    gradz_heads = grad_z.reshape(tok_rows, head_count, E)
    query_wide = query_heads.astype(jnp.float32)
    key_wide = key_heads.astype(jnp.float32)
    value_wide = value_heads.astype(jnp.float32)
    causal = (
        lax.broadcasted_iota(jnp.int32, (tok_rows, tok_rows), 0)
        >= lax.broadcasted_iota(jnp.int32, (tok_rows, tok_rows), 1)
    )[None]
    scores = jnp.einsum("thd,shd->hts", query_heads, key_heads, preferred_element_type=jnp.float32)
    weights = jnp.where(causal, scores, 0.0)
    local_state = jnp.einsum(
        "shd,she->hde", key_heads, value_heads, preferred_element_type=jnp.float32
    )
    state_in = ctx_scan(local_state, False)
    attended = jnp.einsum("hts,she->the", weights, value_wide, precision=highest)
    attended = attended + jnp.einsum("thd,hde->the", query_wide, state_in, precision=highest)
    inv_rms = lax.rsqrt(jnp.mean(attended * attended, axis=-1, keepdims=True) + epsilon)
    normed = attended * inv_rms
    grad_att = (
        inv_rms * (gradz_heads - normed * jnp.mean(gradz_heads * normed, axis=-1, keepdims=True))
    ).astype(jnp.bfloat16)
    grad_wide = grad_att.astype(jnp.float32)
    grad_weights = jnp.where(
        causal,
        jnp.einsum("the,she->hts", grad_att, value_heads, preferred_element_type=jnp.float32),
        0.0,
    )
    grad_query = jnp.einsum("hts,shd->thd", grad_weights, key_wide, precision=highest)
    grad_query = grad_query + jnp.einsum("the,hde->thd", grad_wide, state_in, precision=highest)
    local_adjoint = jnp.einsum(
        "thd,the->hde", query_heads, grad_att, preferred_element_type=jnp.float32
    )
    adjoint = merged_scan(local_adjoint, True)
    grad_key = jnp.einsum("hts,thd->shd", grad_weights, query_wide, precision=highest)
    grad_key = grad_key + jnp.einsum("she,hde->shd", value_wide, adjoint, precision=highest)
    grad_value = jnp.einsum("hts,the->she", weights, grad_wide, precision=highest)
    grad_value = grad_value + jnp.einsum("shd,hde->she", key_wide, adjoint, precision=highest)
    return (
        grad_query.reshape(tok_rows, feat_width).astype(jnp.bfloat16),
        grad_key.reshape(tok_rows, feat_width).astype(jnp.bfloat16),
        grad_value.reshape(tok_rows, feat_width).astype(jnp.bfloat16),
    )


def solution(mesh):
    ctx_size, tp_size = mesh.devices.shape
    chips_y = 2
    fine = Mesh(
        mesh.devices.reshape(chips_y, ctx_size // (2 * chips_y), 2, tp_size // 4, 4),
        CTX + TP,
    )
    return jax.shard_map(
        local,
        mesh=fine,
        in_specs=(P(CTX, TP), P(CTX, TP), P(CTX, TP), P(CTX, TP), P(TP, CTX)),
        out_specs=(P(CTX, TP), P(CTX, TP), P(CTX, TP)),
        check_vma=False,
    )
```

```python
import jax
import jax.numpy as jnp
from jax import lax
from jax.experimental.layout import Layout, with_layout_constraint
from jax.sharding import Mesh
from jax.sharding import PartitionSpec as P

E = 128


epsilon = 1e-06
highest = lax.Precision.HIGHEST

CTX = ("ylo", "z", "core")
TP = ("x", "yhi")
CHIPS = ("ylo", "z")


def swap_cores(value):
    return lax.ppermute(value, "core", [(0, 1), (1, 0)])


def ctx_scan(local_state, backward):
    core = lax.axis_index("core")
    other = swap_cores(local_state)
    first = jnp.where(core == 0, local_state, other)
    second = jnp.where(core == 0, other, local_state)
    chip_total = first + second
    if backward:
        within = jnp.where(core == 0, other, jnp.zeros_like(other))
    else:
        within = jnp.where(core == 1, other, jnp.zeros_like(other))
    half = lax.dynamic_index_in_dim(chip_total, core, 0, keepdims=False)
    chips = lax.axis_size("ylo") * lax.axis_size("z")
    window = half
    below = jnp.zeros_like(half)
    distance = 1
    while distance < chips:
        if backward:
            pairs = [(q, q - distance) for q in range(distance, chips)]
        else:
            pairs = [(q, q + distance) for q in range(chips - distance)]
        arrived = lax.ppermute(window, CHIPS, pairs)
        below = below + arrived
        if distance * 2 < chips:
            window = window + arrived
        distance *= 2
    other_half = swap_cores(below)
    head0 = jnp.where(core == 0, below, other_half)
    head1 = jnp.where(core == 0, other_half, below)
    return jnp.stack([head0, head1]) + within


def gather_columns(w_block):
    chips = lax.axis_size("ylo") * lax.axis_size("z")
    spread = jnp.broadcast_to(w_block[None], (chips,) + w_block.shape)
    mine = lax.all_to_all(spread, CHIPS, 0, 0, tiled=True)
    others = swap_cores(mine)
    core = lax.axis_index("core")
    even = jnp.where(core == 0, mine, others)
    odd = jnp.where(core == 0, others, mine)
    return jnp.stack([even, odd], axis=1)


def local(query, key_feat, value, grad_out, w_out):
    tok_rows = query.shape[0]
    feat_width = query.shape[1]
    head_count = feat_width // E
    full_rows = lax.all_gather(grad_out, TP, axis=1, tiled=True)
    columns = gather_columns(w_out)
    grad_z = jnp.einsum(
        "tqrk,qrjk->tj",
        full_rows.reshape(tok_rows, columns.shape[0], 2, columns.shape[3]),
        columns,
        preferred_element_type=jnp.float32,
    )
    query_heads = query.reshape(tok_rows, head_count, E)
    key_heads = key_feat.reshape(tok_rows, head_count, E)
    value_heads = value.reshape(tok_rows, head_count, E)
    gradz_heads = grad_z.reshape(tok_rows, head_count, E)
    query_wide = query_heads.astype(jnp.float32)
    key_wide = key_heads.astype(jnp.float32)
    value_wide = value_heads.astype(jnp.float32)
    causal = (
        lax.broadcasted_iota(jnp.int32, (tok_rows, tok_rows), 0)
        >= lax.broadcasted_iota(jnp.int32, (tok_rows, tok_rows), 1)
    )[None]
    scores = jnp.einsum("thd,shd->hts", query_heads, key_heads, preferred_element_type=jnp.float32)
    weights = jnp.where(causal, scores, 0.0)
    local_state = jnp.einsum(
        "shd,she->hde", key_heads, value_heads, preferred_element_type=jnp.float32
    )
    state_in = ctx_scan(local_state, False)
    attended = jnp.einsum("hts,she->the", weights, value_wide, precision=highest)
    attended = attended + jnp.einsum("thd,hde->the", query_wide, state_in, precision=highest)
    inv_rms = lax.rsqrt(jnp.mean(attended * attended, axis=-1, keepdims=True) + epsilon)
    normed = attended * inv_rms
    grad_att = (
        inv_rms * (gradz_heads - normed * jnp.mean(gradz_heads * normed, axis=-1, keepdims=True))
    ).astype(jnp.bfloat16)
    grad_wide = grad_att.astype(jnp.float32)
    grad_weights = jnp.where(
        causal,
        jnp.einsum("the,she->hts", grad_att, value_heads, preferred_element_type=jnp.float32),
        0.0,
    )
    grad_query = jnp.einsum("hts,shd->thd", grad_weights, key_wide, precision=highest)
    grad_query = grad_query + jnp.einsum("the,hde->thd", grad_wide, state_in, precision=highest)
    local_adjoint = jnp.einsum(
        "thd,the->hde", query_heads, grad_att, preferred_element_type=jnp.float32
    )
    adjoint = ctx_scan(local_adjoint, True)
    grad_key = jnp.einsum("hts,thd->shd", grad_weights, query_wide, precision=highest)
    grad_key = grad_key + jnp.einsum("she,hde->shd", value_wide, adjoint, precision=highest)
    grad_value = jnp.einsum("hts,the->she", weights, grad_wide, precision=highest)
    grad_value = grad_value + jnp.einsum("shd,hde->she", key_wide, adjoint, precision=highest)
    row_major = Layout(major_to_minor=(0, 1))
    return tuple(
        with_layout_constraint(out.reshape(tok_rows, feat_width), row_major).astype(jnp.bfloat16)
        for out in (grad_query, grad_key, grad_value)
    )


def solution(mesh):
    ctx_size, tp_size = mesh.devices.shape
    chips_y = 2
    fine = Mesh(
        mesh.devices.reshape(chips_y, ctx_size // (2 * chips_y), 2, tp_size // 4, 4),
        CTX + TP,
    )
    return jax.shard_map(
        local,
        mesh=fine,
        in_specs=(P(CTX, TP), P(CTX, TP), P(CTX, TP), P(CTX, TP), P(TP, CTX)),
        out_specs=(P(CTX, TP), P(CTX, TP), P(CTX, TP)),
        check_vma=False,
    )
```

```python
import jax
import jax.numpy as jnp
from jax import lax
from jax.experimental.layout import Layout, with_layout_constraint
from jax.sharding import Mesh
from jax.sharding import PartitionSpec as P

E = 128


epsilon = 1e-06
highest = lax.Precision.HIGHEST

CTX = ("ylo", "z", "core")
TP = ("x", "yhi")
CHIPS = ("ylo", "z")


def swap_cores(value):
    return lax.ppermute(value, "core", [(0, 1), (1, 0)])


def ctx_scan(local_state, backward):
    core = lax.axis_index("core")
    other = swap_cores(local_state)
    first = jnp.where(core == 0, local_state, other)
    second = jnp.where(core == 0, other, local_state)
    chip_total = first + second
    if backward:
        within = jnp.where(core == 0, other, jnp.zeros_like(other))
    else:
        within = jnp.where(core == 1, other, jnp.zeros_like(other))
    half = lax.dynamic_index_in_dim(chip_total, core, 0, keepdims=False)
    chips = lax.axis_size("ylo") * lax.axis_size("z")
    window = half
    below = jnp.zeros_like(half)
    distance = 1
    while distance < chips:
        if backward:
            pairs = [(q, q - distance) for q in range(distance, chips)]
        else:
            pairs = [(q, q + distance) for q in range(chips - distance)]
        arrived = lax.ppermute(window, CHIPS, pairs)
        below = below + arrived
        if distance * 2 < chips:
            window = window + arrived
        distance *= 2
    other_half = swap_cores(below)
    head0 = jnp.where(core == 0, below, other_half)
    head1 = jnp.where(core == 0, other_half, below)
    return jnp.stack([head0, head1]) + within


def gather_columns(w_block):
    chips = lax.axis_size("ylo") * lax.axis_size("z")
    spread = jnp.broadcast_to(w_block[None], (chips,) + w_block.shape)
    mine = lax.all_to_all(spread, CHIPS, 0, 0, tiled=True)
    others = swap_cores(mine)
    core = lax.axis_index("core")
    even = jnp.where(core == 0, mine, others)
    odd = jnp.where(core == 0, others, mine)
    return jnp.stack([even, odd], axis=1)


def local(query, key_feat, value, grad_out, w_out):
    tok_rows = query.shape[0]
    feat_width = query.shape[1]
    head_count = feat_width // E
    full_rows = lax.all_gather(grad_out, TP, axis=0)
    columns = gather_columns(w_out)
    grad_z = jnp.einsum(
        "qtrk,qrjk->tj",
        full_rows.reshape(columns.shape[0], tok_rows, 2, columns.shape[3]),
        columns,
        preferred_element_type=jnp.float32,
    )
    query_heads = query.reshape(tok_rows, head_count, E)
    key_heads = key_feat.reshape(tok_rows, head_count, E)
    value_heads = value.reshape(tok_rows, head_count, E)
    gradz_heads = grad_z.reshape(tok_rows, head_count, E)
    query_wide = query_heads.astype(jnp.float32)
    key_wide = key_heads.astype(jnp.float32)
    value_wide = value_heads.astype(jnp.float32)
    causal = (
        lax.broadcasted_iota(jnp.int32, (tok_rows, tok_rows), 0)
        >= lax.broadcasted_iota(jnp.int32, (tok_rows, tok_rows), 1)
    )[None]
    scores = jnp.einsum("thd,shd->hts", query_heads, key_heads, preferred_element_type=jnp.float32)
    weights = jnp.where(causal, scores, 0.0)
    local_state = jnp.einsum(
        "shd,she->hde", key_heads, value_heads, preferred_element_type=jnp.float32
    )
    state_in = ctx_scan(local_state, False)
    attended = jnp.einsum("hts,she->the", weights, value_wide, precision=highest)
    attended = attended + jnp.einsum("thd,hde->the", query_wide, state_in, precision=highest)
    inv_rms = lax.rsqrt(jnp.mean(attended * attended, axis=-1, keepdims=True) + epsilon)
    normed = attended * inv_rms
    grad_att = (
        inv_rms * (gradz_heads - normed * jnp.mean(gradz_heads * normed, axis=-1, keepdims=True))
    ).astype(jnp.bfloat16)
    grad_wide = grad_att.astype(jnp.float32)
    grad_weights = jnp.where(
        causal,
        jnp.einsum("the,she->hts", grad_att, value_heads, preferred_element_type=jnp.float32),
        0.0,
    )
    grad_query = jnp.einsum("hts,shd->thd", grad_weights, key_wide, precision=highest)
    grad_query = grad_query + jnp.einsum("the,hde->thd", grad_wide, state_in, precision=highest)
    local_adjoint = jnp.einsum(
        "thd,the->hde", query_heads, grad_att, preferred_element_type=jnp.float32
    )
    adjoint = ctx_scan(local_adjoint, True)
    grad_key = jnp.einsum("hts,thd->shd", grad_weights, query_wide, precision=highest)
    grad_key = grad_key + jnp.einsum("she,hde->shd", value_wide, adjoint, precision=highest)
    grad_value = jnp.einsum("hts,the->she", weights, grad_wide, precision=highest)
    grad_value = grad_value + jnp.einsum("shd,hde->she", key_wide, adjoint, precision=highest)
    row_major = Layout(major_to_minor=(0, 1))
    return tuple(
        with_layout_constraint(out.reshape(tok_rows, feat_width), row_major).astype(jnp.bfloat16)
        for out in (grad_query, grad_key, grad_value)
    )


def solution(mesh):
    ctx_size, tp_size = mesh.devices.shape
    chips_y = 2
    fine = Mesh(
        mesh.devices.reshape(chips_y, ctx_size // (2 * chips_y), 2, tp_size // 4, 4),
        CTX + TP,
    )
    return jax.shard_map(
        local,
        mesh=fine,
        in_specs=(P(CTX, TP), P(CTX, TP), P(CTX, TP), P(CTX, TP), P(TP, CTX)),
        out_specs=(P(CTX, TP), P(CTX, TP), P(CTX, TP)),
        check_vma=False,
    )
```

```python
import jax
import jax.numpy as jnp
from jax import lax
from jax.experimental.layout import Layout, with_layout_constraint
from jax.sharding import Mesh
from jax.sharding import PartitionSpec as P

E = 128


epsilon = 1e-06
highest = lax.Precision.HIGHEST

CTX = ("ylo", "z", "core")
TP = ("x", "yhi")
CHIPS = ("ylo", "z")


def swap_cores(value):
    return lax.ppermute(value, "core", [(0, 1), (1, 0)])


def ctx_scan(local_state, backward):
    core = lax.axis_index("core")
    other = swap_cores(local_state)
    first = jnp.where(core == 0, local_state, other)
    second = jnp.where(core == 0, other, local_state)
    chip_total = first + second
    if backward:
        within = jnp.where(core == 0, other, jnp.zeros_like(other))
    else:
        within = jnp.where(core == 1, other, jnp.zeros_like(other))
    half = lax.dynamic_index_in_dim(chip_total, core, 0, keepdims=False)
    chips = lax.axis_size("ylo") * lax.axis_size("z")
    window = half
    below = jnp.zeros_like(half)
    distance = 1
    while distance < chips:
        if backward:
            pairs = [(q, q - distance) for q in range(distance, chips)]
        else:
            pairs = [(q, q + distance) for q in range(chips - distance)]
        arrived = lax.ppermute(window, CHIPS, pairs)
        below = below + arrived
        if distance * 2 < chips:
            window = window + arrived
        distance *= 2
    other_half = swap_cores(below)
    head0 = jnp.where(core == 0, below, other_half)
    head1 = jnp.where(core == 0, other_half, below)
    return jnp.stack([head0, head1]) + within


def merged_scan(local_state, backward):
    core = lax.axis_index("core")
    chips = lax.axis_size("ylo") * lax.axis_size("z")
    step = -1 if backward else 1
    nearest = [(q, q + step) for q in range(chips) if 0 <= q + step < chips]
    other = swap_cores(local_state)
    own_head = lax.dynamic_index_in_dim(local_state, core, 0, keepdims=False)
    cross_head = lax.dynamic_index_in_dim(local_state, 1 - core, 0, keepdims=False)
    same = lax.ppermute(own_head, CHIPS, nearest)
    cross = lax.ppermute(
        cross_head, CTX, [(2 * q + c, 2 * t + 1 - c) for q, t in nearest for c in (0, 1)]
    )
    below = jnp.where(core == 0, same + cross, cross + same)
    paired = lax.dynamic_index_in_dim(other, core, 0, keepdims=False)
    window = jnp.where(core == 0, own_head + paired, paired + own_head) + below
    if backward:
        within = jnp.where(core == 0, other, jnp.zeros_like(other))
    else:
        within = jnp.where(core == 1, other, jnp.zeros_like(other))
    distance = 2
    while distance < chips:
        pairs = [(q, q + step * distance) for q in range(chips) if 0 <= q + step * distance < chips]
        arrived = lax.ppermute(window, CHIPS, pairs)
        below = below + arrived
        if distance * 2 < chips:
            window = window + arrived
        distance *= 2
    other_half = swap_cores(below)
    head0 = jnp.where(core == 0, below, other_half)
    head1 = jnp.where(core == 0, other_half, below)
    return jnp.stack([head0, head1]) + within


def gather_columns(w_block):
    chips = lax.axis_size("ylo") * lax.axis_size("z")
    spread = jnp.broadcast_to(w_block[None], (chips,) + w_block.shape)
    mine = lax.all_to_all(spread, CHIPS, 0, 0, tiled=True)
    others = swap_cores(mine)
    core = lax.axis_index("core")
    even = jnp.where(core == 0, mine, others)
    odd = jnp.where(core == 0, others, mine)
    return jnp.stack([even, odd], axis=1)


def local(query, key_feat, value, grad_out, w_out):
    tok_rows = query.shape[0]
    feat_width = query.shape[1]
    head_count = feat_width // E
    full_rows = lax.all_gather(grad_out, TP, axis=1, tiled=True)
    columns = gather_columns(w_out)
    grad_z = jnp.einsum(
        "tqrk,qrjk->tj",
        full_rows.reshape(tok_rows, columns.shape[0], 2, columns.shape[3]),
        columns,
        preferred_element_type=jnp.float32,
    )
    query_heads = query.reshape(tok_rows, head_count, E)
    key_heads = key_feat.reshape(tok_rows, head_count, E)
    value_heads = value.reshape(tok_rows, head_count, E)
    gradz_heads = grad_z.reshape(tok_rows, head_count, E)
    query_wide = query_heads.astype(jnp.float32)
    key_wide = key_heads.astype(jnp.float32)
    value_wide = value_heads.astype(jnp.float32)
    causal = (
        lax.broadcasted_iota(jnp.int32, (tok_rows, tok_rows), 0)
        >= lax.broadcasted_iota(jnp.int32, (tok_rows, tok_rows), 1)
    )[None]
    scores = jnp.einsum("thd,shd->hts", query_heads, key_heads, preferred_element_type=jnp.float32)
    weights = jnp.where(causal, scores, 0.0)
    local_state = jnp.einsum(
        "shd,she->hde", key_heads, value_heads, preferred_element_type=jnp.float32
    )
    state_in = ctx_scan(local_state, False)
    attended = jnp.einsum("hts,she->the", weights, value_wide, precision=highest)
    attended = attended + jnp.einsum("thd,hde->the", query_wide, state_in, precision=highest)
    inv_rms = lax.rsqrt(jnp.mean(attended * attended, axis=-1, keepdims=True) + epsilon)
    normed = attended * inv_rms
    grad_att = (
        inv_rms * (gradz_heads - normed * jnp.mean(gradz_heads * normed, axis=-1, keepdims=True))
    ).astype(jnp.bfloat16)
    grad_wide = grad_att.astype(jnp.float32)
    grad_weights = jnp.where(
        causal,
        jnp.einsum("the,she->hts", grad_att, value_heads, preferred_element_type=jnp.float32),
        0.0,
    )
    grad_query = jnp.einsum("hts,shd->thd", grad_weights, key_wide, precision=highest)
    grad_query = grad_query + jnp.einsum("the,hde->thd", grad_wide, state_in, precision=highest)
    local_adjoint = jnp.einsum(
        "thd,the->hde", query_heads, grad_att, preferred_element_type=jnp.float32
    )
    adjoint = merged_scan(local_adjoint, True)
    grad_key = jnp.einsum("hts,thd->shd", grad_weights, query_wide, precision=highest)
    grad_key = grad_key + jnp.einsum("she,hde->shd", value_wide, adjoint, precision=highest)
    grad_value = jnp.einsum("hts,the->she", weights, grad_wide, precision=highest)
    grad_value = grad_value + jnp.einsum("shd,hde->she", key_wide, adjoint, precision=highest)
    row_major = Layout(major_to_minor=(0, 1))
    return tuple(
        with_layout_constraint(out.reshape(tok_rows, feat_width), row_major).astype(jnp.bfloat16)
        for out in (grad_query, grad_key, grad_value)
    )


def solution(mesh):
    ctx_size, tp_size = mesh.devices.shape
    chips_y = 2
    fine = Mesh(
        mesh.devices.reshape(chips_y, ctx_size // (2 * chips_y), 2, tp_size // 4, 4),
        CTX + TP,
    )
    return jax.shard_map(
        local,
        mesh=fine,
        in_specs=(P(CTX, TP), P(CTX, TP), P(CTX, TP), P(CTX, TP), P(TP, CTX)),
        out_specs=(P(CTX, TP), P(CTX, TP), P(CTX, TP)),
        check_vma=False,
    )
```
